512 devices in a mesh: dp: 8 (over y_lo, core), gx: 64 (over y_hi, z, x).
Axes of the slice: x: 4, y: 8 (y_hi: 2, y_lo: 4; y = y_hi * 4 + y_lo), z: 8, core: 2. Of those that a mesh axis runs over, the one named last changes fastest.
Arguments:
- features: bfloat16 [8, 16, 128, 8, 256], P('dp', None, 'gx'), may hold values from -6 to 6
- offsets: int32 [8, 3], P('dp'), may hold values from 0 to 255, as said below
- flip_bits: int32 [8, 3], P('dp'), may hold values from 0 to 1
- weight: bfloat16 [27, 16, 16], replicated, may hold values from -0.3125 to 0.3125
- conv_bias: float32 [16], replicated, may hold values from -3 to 3
- cotangent: bfloat16 [8, 16, 128, 8, 256], P('dp', None, 'gx'), may hold values from -6 to 6
Outputs:
- hidden: bfloat16 [8, 16, 128, 8, 256], P('dp', None, 'gx')
- grad_input: bfloat16 [8, 16, 128, 8, 256], P('dp', None, 'gx')
- grad_weight: float32 [27, 16, 16], replicated
- grad_bias: float32 [16], replicated
The draws below stay inside these ranges and needn't reach their ends.
Inputs may be any that keep to these rules, and one draw needn't show every extreme that they name: `offsets`: column 0 lies in 0 to 127, column 1 in 0 to 7, column 2 in 0 to 255.
All inputs are finite; a program needn't handle non-finite values.
Results may differ from the reference program's by a relative error of at most 0.0075.
Values may be sent and summed in bfloat16 or wider, within the bound.
No kernel may reach another device: no remote copies, remote signals or barrier semaphores. Data moves between devices by JAX's collectives and lax.ppermute only.
A program may use at most 64 MiB of HBM per device.

```python
import math
import jax
import jax.numpy as jnp
from jax import lax

CH = 16
NY = 8
NZ = 256
NX = 128
FIELDS = 8


def draw_offsets(key, part):
    limits = jnp.array([NX, NY, NZ], dtype=jnp.int32)
    drawn = jax.random.randint(jax.random.fold_in(key, 1), (FIELDS, 3), 0, limits, dtype=jnp.int32)
    field_high = jax.random.randint(jax.random.fold_in(key, 2), (), 0, FIELDS, dtype=jnp.int32)
    field_low = jnp.mod(field_high + 1, FIELDS).astype(jnp.int32)
    rows = jnp.arange(FIELDS, dtype=jnp.int32)[:, None]
    columns = jnp.arange(3, dtype=jnp.int32)[None, :]
    drawn = jnp.where(rows == field_high, (limits - 1)[None, :], drawn)
    drawn = jnp.where((rows == field_low) & (columns == 2), jnp.zeros_like(drawn), drawn)
    return drawn.astype(jnp.int32)


def touch_ends(values, rng, smallest, high):
    place = [jax.random.randint(jax.random.fold_in(rng, axis), (), 0, length) for axis, length in enumerate(values.shape)]
    longest = values.shape.index(max(values.shape))
    next_to = place[:longest] + [(place[longest] + 1) % values.shape[longest]] + place[longest + 1:]
    return values.at[tuple(place)].set(smallest).at[tuple(next_to)].set(high)


def steps_of(own_key, extent, shards, least, largest):
    gain = 1.0
    for dim, blocks in shards:
        draws = jax.random.uniform(jax.random.fold_in(jax.random.fold_in(own_key, 6), dim), (blocks,), jnp.float32, least / len(shards), largest / len(shards))
        gain = gain * jnp.repeat(jnp.exp(draws), extent[dim] // blocks).reshape((-1,) + (1,) * (len(extent) - 1 - dim))
    return gain


def bell_draw(stream_key, dims, deviation, most, pieces=(), kind=jnp.bfloat16):
    result = jax.random.normal(stream_key, dims, jnp.float32) * deviation
    if len(pieces) > 0:
        result = steps_of(stream_key, dims, pieces, -0.22, 0.18) * result
    return jnp.clip(result, min=-most, max=most).astype(kind)


def setup_inputs(seed: int = 0) -> dict:
    key_list = jax.random.split(jax.random.key(seed), 7)
    return {
        "features": bell_draw(key_list[0], (FIELDS, CH, NX, NY, NZ), 1.0, 6.0, ((0, 8), (2, 64))),
        "offsets": draw_offsets(jax.random.fold_in(key_list[6], 71), 0),
        "flip_bits": touch_ends(jax.random.randint(key_list[2], (FIELDS, 3), 0, 2), jax.random.fold_in(key_list[2], 1), 0, 1).astype(jnp.int32),
        "weight": bell_draw(key_list[3], (27, CH, CH), (27 * CH) ** -0.5, 0.3125),
        "conv_bias": bell_draw(key_list[4], (CH,), 0.5, 3.0, (), jnp.float32),
        "cotangent": bell_draw(key_list[5], (FIELDS, CH, NX, NY, NZ), 1.0, 6.0, ((0, 8), (2, 64))),
    }


tap_offsets = [(shift_x, shift_y, shift_z) for shift_x in range(3) for shift_y in range(3) for shift_z in range(3)]

def permute_axis(volume, offset, mirror_bit, length, dim_index):
    position = jnp.arange(length, dtype=jnp.int32)
    source = jnp.where(mirror_bit == 1, length - 1 - position, position)
    source = jnp.mod(source - offset, length).astype(jnp.int32)
    return jnp.take(volume, source, axis=dim_index)

def gelu_parts(pre_act):
    normal_cdf = 0.5 * (1.0 + lax.erf(pre_act * 0.7071067811865476))
    density = jnp.exp(-0.5 * pre_act * pre_act) * 0.3989422804014327
    return (pre_act * normal_cdf, normal_cdf + pre_act * density)

def one_field(volume, offset, mirror_bits, cotangent, weight, conv_bias):
    augmented = permute_axis(volume, offset[0], mirror_bits[0], NX, 1)
    augmented = permute_axis(augmented, offset[1], mirror_bits[1], NY, 2)
    augmented = permute_axis(augmented, offset[2], mirror_bits[2], NZ, 3)
    augmented32 = augmented.astype(jnp.float32)
    weights32 = weight.astype(jnp.float32)
    total = jnp.zeros(augmented32.shape, jnp.float32) + conv_bias.astype(jnp.float32)[:, None, None, None]
    for tap_index, (shift_x, shift_y, shift_z) in enumerate(tap_offsets):
        window = jnp.roll(augmented32, (1 - shift_x, 1 - shift_y, 1 - shift_z), axis=(1, 2, 3))
        total = total + jnp.einsum('oi,ixyz->oxyz', weights32[tap_index], window)
    hidden, slope = gelu_parts(total)
    grad_pre = (cotangent.astype(jnp.float32) * slope).astype(jnp.bfloat16)
    grad32 = grad_pre.astype(jnp.float32)
    grad_in = jnp.zeros(augmented32.shape, jnp.float32)
    grad_list = []
    for tap_index, (shift_x, shift_y, shift_z) in enumerate(tap_offsets):
        window = jnp.roll(augmented32, (1 - shift_x, 1 - shift_y, 1 - shift_z), axis=(1, 2, 3))
        grad_list.append(jnp.einsum('oxyz,ixyz->oi', grad32, window))
        moved_grad = jnp.roll(grad32, (shift_x - 1, shift_y - 1, shift_z - 1), axis=(1, 2, 3))
        grad_in = grad_in + jnp.einsum('oi,oxyz->ixyz', weights32[tap_index], moved_grad)
    return (hidden.astype(jnp.bfloat16), grad_in.astype(jnp.bfloat16), jnp.stack(grad_list), lax.optimization_barrier(jnp.sum(grad32, axis=(1, 2, 3))))

def reference(features, offsets, flip_bits, weight, conv_bias, cotangent):

    def run_field(items):
        return one_field(items[0], items[1], items[2], items[3], weight, conv_bias)
    hidden, grad_input, grad_w, grad_b = lax.map(run_field, (features, offsets, flip_bits, cotangent))
    grad_scale = 1.0 / math.sqrt(FIELDS * NX * NY * NZ)
    return (hidden, grad_input, lax.optimization_barrier(jnp.sum(grad_w, axis=0)) * grad_scale, lax.optimization_barrier(jnp.sum(grad_b, axis=0)) * grad_scale)
```

```python
import math

import jax
import jax.numpy as jnp
from jax import lax
from jax.sharding import PartitionSpec as P

tap_offsets = [
    (shift_x, shift_y, shift_z)
    for shift_x in range(3)
    for shift_y in range(3)
    for shift_z in range(3)
]


def shifted(value, axis, steps):
    count = lax.axis_size(axis)
    pairs = [(source, (source + steps) % count) for source in range(count)]
    return lax.ppermute(value, axis, pairs)


def mirrored_of(value, axis):
    count = lax.axis_size(axis)
    pairs = [(source, count - 1 - source) for source in range(count)]
    return lax.ppermute(value, axis, pairs)


def butterfly_sum(value, axis):
    count = lax.axis_size(axis)
    step = 1
    while step < count:
        pairs = [(source, source ^ step) for source in range(count)]
        value = value + lax.ppermute(value, axis, pairs)
        step *= 2
    return value


def permute_axis(volume, offset, mirror_bit, length, dim_index):
    position = jnp.arange(length, dtype=jnp.int32)
    source = jnp.where(mirror_bit == 1, length - 1 - position, position)
    source = jnp.mod(source - offset, length)
    return jnp.take(volume, source, axis=dim_index)


def augment_local(volume, offset, mirror_bits):
    volume = permute_axis(volume, offset[1], mirror_bits[1], volume.shape[2], 2)
    return permute_axis(volume, offset[2], mirror_bits[2], volume.shape[3], 3)


def gelu_parts(pre_act):
    normal_cdf = 0.5 * (1.0 + lax.erf(pre_act * 0.7071067811865476))
    density = jnp.exp(-0.5 * pre_act * pre_act) * 0.3989422804014327
    return (pre_act * normal_cdf, normal_cdf + pre_act * density)


def windows(padded, planes, sign):
    out = []
    for shift_x, shift_y, shift_z in tap_offsets:
        start = shift_x if sign > 0 else 2 - shift_x
        piece = padded[:, :, start : start + planes]
        out.append(jnp.roll(piece, (sign * (1 - shift_y), sign * (1 - shift_z)), axis=(3, 4)))
    return jnp.stack(out, 0)


def on_device(features, offsets, flip_bits, weight, conv_bias, cotangent):
    planes = features.shape[2]
    devices_x = lax.axis_size("gx")
    levels = devices_x.bit_length() - 1
    length_x = planes * devices_x
    local = jax.vmap(augment_local)(features, offsets, flip_bits)
    flip_x = flip_bits[0, 0] == 1
    reversed_local = jnp.flip(local, 2)
    mirrored = jnp.where(flip_x, mirrored_of(reversed_local, "gx"), local)
    effective = jnp.where(flip_x, jnp.mod(-offsets[0, 0], length_x), offsets[0, 0])
    coarse_steps = effective // planes
    remain = effective % planes
    coarse = mirrored
    for bit_level in range(levels):
        arrived = shifted(coarse, "gx", 2**bit_level)
        coarse = jnp.where(coarse_steps // 2**bit_level % 2 == 1, arrived, coarse)
    before = shifted(coarse, "gx", 1)
    after = shifted(coarse, "gx", -1)
    joined = jnp.concatenate([before, coarse, after], axis=2)
    padded = lax.dynamic_slice_in_dim(joined, planes - 1 - remain, planes + 2, axis=2)

    taps = len(tap_offsets)
    channels = features.shape[1]
    flat_weight = weight.reshape(taps, channels, channels)
    cols = windows(padded, planes, 1)
    total = jnp.einsum(
        "toi,tbixyz->boxyz", flat_weight, cols, preferred_element_type=jnp.float32
    ) + conv_bias[None, :, None, None, None]
    hidden, slope = gelu_parts(total)
    grad_pre = (cotangent.astype(jnp.float32) * slope).astype(jnp.bfloat16)
    grad_before = shifted(grad_pre[:, :, planes - 1 : planes], "gx", 1)
    grad_after = shifted(grad_pre[:, :, 0:1], "gx", -1)
    grad_w = jnp.einsum("boxyz,tbixyz->toi", grad_pre, cols, preferred_element_type=jnp.float32)
    grad_b = jnp.sum(grad_pre.astype(jnp.float32), axis=(0, 2, 3, 4))
    stacked = jnp.concatenate([grad_w.reshape(-1), grad_b])
    summed = butterfly_sum(butterfly_sum(stacked, "dp"), "gx")
    grad_pad = jnp.concatenate([grad_before, grad_pre, grad_after], axis=2)
    moved = windows(grad_pad, planes, -1)
    grad_in = jnp.einsum(
        "toi,tboxyz->bixyz", flat_weight, moved, preferred_element_type=jnp.float32
    )
    cell_count = (
        features.shape[0] * lax.axis_size("dp") * length_x * features.shape[3] * features.shape[4]
    )
    grad_scale = 1.0 / math.sqrt(cell_count)
    summed = summed * grad_scale
    weight_count = taps * channels * channels
    return (
        hidden.astype(jnp.bfloat16),
        grad_in.astype(jnp.bfloat16),
        summed[:weight_count].reshape(taps, channels, channels),
        summed[weight_count:],
    )


def solution(mesh):
    in_specs = (
        P("dp", None, "gx", None, None),
        P("dp", None),
        P("dp", None),
        P(),
        P(),
        P("dp", None, "gx", None, None),
    )
    out_specs = (P("dp", None, "gx", None, None), P("dp", None, "gx", None, None), P(), P())
    return jax.shard_map(
        on_device, mesh=mesh, in_specs=in_specs, out_specs=out_specs, check_vma=False
    )
```

```python
import math

import jax
import jax.numpy as jnp
from jax import lax
from jax.sharding import PartitionSpec as P

tap_offsets = [
    (shift_x, shift_y, shift_z)
    for shift_x in range(3)
    for shift_y in range(3)
    for shift_z in range(3)
]


def shifted(value, axis, steps):
    count = lax.axis_size(axis)
    pairs = [(source, (source + steps) % count) for source in range(count)]
    return lax.ppermute(value, axis, pairs)


def butterfly_sum(value, axis):
    count = lax.axis_size(axis)
    step = 1
    while step < count:
        pairs = [(source, source ^ step) for source in range(count)]
        value = value + lax.ppermute(value, axis, pairs)
        step *= 2
    return value


def permute_axis(volume, offset, mirror_bit, length, dim_index):
    position = jnp.arange(length, dtype=jnp.int32)
    source = jnp.where(mirror_bit == 1, length - 1 - position, position)
    source = jnp.mod(source - offset, length)
    return jnp.take(volume, source, axis=dim_index)


def augment_local(volume, offset, mirror_bits):
    volume = permute_axis(volume, offset[1], mirror_bits[1], volume.shape[2], 2)
    return permute_axis(volume, offset[2], mirror_bits[2], volume.shape[3], 3)


def gelu_parts(pre_act):
    normal_cdf = 0.5 * (1.0 + lax.erf(pre_act * 0.7071067811865476))
    density = jnp.exp(-0.5 * pre_act * pre_act) * 0.3989422804014327
    return (pre_act * normal_cdf, normal_cdf + pre_act * density)


def circular_yz(volume):
    volume = jnp.concatenate([volume[:, :, :, -1:], volume, volume[:, :, :, :1]], axis=3)
    return jnp.concatenate([volume[..., -1:], volume, volume[..., :1]], axis=4)


def conv3(lhs, rhs, numbers):
    return lax.conv_general_dilated(
        lhs, rhs, (1, 1, 1), "VALID", dimension_numbers=numbers,
        preferred_element_type=jnp.float32,
    )


def routed(value, axis, sign, constant):
    count = lax.axis_size(axis)
    here = lax.axis_index(axis)
    step = 1
    while step < count:
        low = jnp.mod(sign * (here - constant), step)
        source = here // (2 * step) * (2 * step) + here % (2 * step) // step * step + low
        target = jnp.mod(sign * source + constant, count)
        swap = (source // step % 2) != (target // step % 2)
        pairs = [(peer, peer ^ step) for peer in range(count)]
        value = jnp.where(swap, lax.ppermute(value, axis, pairs), value)
        step *= 2
    return value


def on_device(features, offsets, flip_bits, weight, conv_bias, cotangent):
    planes = features.shape[2]
    devices_x = lax.axis_size("gx")
    length_x = planes * devices_x
    local = jax.vmap(augment_local)(features, offsets, flip_bits)
    flip_x = flip_bits[0, 0] == 1
    block = jnp.where(flip_x, jnp.flip(local, 2), local)
    effective = jnp.where(flip_x, jnp.mod(-offsets[0, 0], length_x), offsets[0, 0])
    coarse_steps = effective // planes
    remain = effective % planes
    sign = jnp.where(flip_x, -1, 1)
    constant = jnp.where(flip_x, devices_x - 1 + coarse_steps, coarse_steps)
    coarse = routed(block, "gx", sign, constant)
    before = shifted(coarse, "gx", 1)
    after = shifted(coarse, "gx", -1)
    joined = jnp.concatenate([before, coarse, after], axis=2)
    padded = lax.dynamic_slice_in_dim(joined, planes - 1 - remain, planes + 2, axis=2)

    taps = len(tap_offsets)
    channels = features.shape[1]
    kernel = weight.reshape(3, 3, 3, channels, channels)
    forward_kernel = jnp.transpose(kernel, (3, 4, 0, 1, 2))
    backward_kernel = jnp.transpose(jnp.flip(kernel, (0, 1, 2)), (4, 3, 0, 1, 2))
    numbers = ("NCDHW", "OIDHW", "NCDHW")
    aug_pad = circular_yz(padded)
    total = conv3(aug_pad, forward_kernel, numbers) + conv_bias[None, :, None, None, None]
    hidden, slope = gelu_parts(total)
    grad_pre = (cotangent.astype(jnp.float32) * slope).astype(jnp.bfloat16)
    grad_before = shifted(grad_pre[:, :, planes - 1 : planes], "gx", 1)
    grad_after = shifted(grad_pre[:, :, 0:1], "gx", -1)
    filter_grad = conv3(aug_pad, grad_pre, ("CNDHW", "IODHW", "NCDHW"))
    grad_w = jnp.transpose(filter_grad, (2, 3, 4, 1, 0)).reshape(-1)
    grad_b = jnp.sum(grad_pre.astype(jnp.float32), axis=(0, 2, 3, 4))
    stacked = jnp.concatenate([grad_w, grad_b])
    summed = butterfly_sum(butterfly_sum(stacked, "dp"), "gx")
    grad_pad = circular_yz(jnp.concatenate([grad_before, grad_pre, grad_after], axis=2))
    grad_in = conv3(grad_pad, backward_kernel, numbers)
    cell_count = (
        features.shape[0] * lax.axis_size("dp") * length_x * features.shape[3] * features.shape[4]
    )
    grad_scale = 1.0 / math.sqrt(cell_count)
    summed = summed * grad_scale
    weight_count = taps * channels * channels
    return (
        hidden.astype(jnp.bfloat16),
        grad_in.astype(jnp.bfloat16),
        summed[:weight_count].reshape(taps, channels, channels),
        summed[weight_count:],
    )


def solution(mesh):
    in_specs = (
        P("dp", None, "gx", None, None),
        P("dp", None),
        P("dp", None),
        P(),
        P(),
        P("dp", None, "gx", None, None),
    )
    out_specs = (P("dp", None, "gx", None, None), P("dp", None, "gx", None, None), P(), P())
    return jax.shard_map(
        on_device, mesh=mesh, in_specs=in_specs, out_specs=out_specs, check_vma=False
    )
```

```python
import math

import jax
import jax.numpy as jnp
from jax import lax
from jax.sharding import PartitionSpec as P

tap_offsets = [
    (shift_x, shift_y, shift_z)
    for shift_x in range(3)
    for shift_y in range(3)
    for shift_z in range(3)
]


def shifted(value, axis, steps):
    count = lax.axis_size(axis)
    pairs = [(source, (source + steps) % count) for source in range(count)]
    return lax.ppermute(value, axis, pairs)


def butterfly_sum(value, axis):
    count = lax.axis_size(axis)
    step = 1
    while step < count:
        pairs = [(source, source ^ step) for source in range(count)]
        value = value + lax.ppermute(value, axis, pairs)
        step *= 2
    return value


def permute_axis(volume, offset, mirror_bit, dim_index):
    reverse = jnp.flip(volume, dim_index)
    return jnp.where(
        mirror_bit == 1,
        jnp.roll(reverse, -offset, axis=dim_index),
        jnp.roll(volume, offset, axis=dim_index),
    )


def augment_local(volume, offset, mirror_bits):
    volume = permute_axis(volume, offset[1], mirror_bits[1], 2)
    return permute_axis(volume, offset[2], mirror_bits[2], 3)


def gelu_parts(pre_act):
    normal_cdf = 0.5 * (1.0 + lax.erf(pre_act * 0.7071067811865476))
    density = jnp.exp(-0.5 * pre_act * pre_act) * 0.3989422804014327
    return (pre_act * normal_cdf, normal_cdf + pre_act * density)


def routed(value, axis, sign, constant):
    count = lax.axis_size(axis)
    here = lax.axis_index(axis)
    step = 1
    while step < count:
        low = jnp.mod(sign * (here - constant), step)
        source = here // (2 * step) * (2 * step) + here % (2 * step) // step * step + low
        target = jnp.mod(sign * source + constant, count)
        swap = (source // step % 2) != (target // step % 2)
        pairs = [(peer, peer ^ step) for peer in range(count)]
        value = jnp.where(swap, lax.ppermute(value, axis, pairs), value)
        step *= 2
    return value


def on_device(features, offsets, flip_bits, weight, conv_bias, cotangent):
    planes = features.shape[2]
    devices_x = lax.axis_size("gx")
    length_x = planes * devices_x
    local = jax.vmap(augment_local)(features, offsets, flip_bits)
    flip_x = flip_bits[0, 0] == 1
    block = jnp.where(flip_x, jnp.flip(local, 2), local)
    effective = jnp.where(flip_x, jnp.mod(-offsets[0, 0], length_x), offsets[0, 0])
    coarse_steps = effective // planes
    remain = effective % planes
    sign = jnp.where(flip_x, -1, 1)
    constant = jnp.where(flip_x, devices_x - 1 + coarse_steps, coarse_steps)
    coarse = routed(block, "gx", sign, constant)
    before = shifted(coarse, "gx", 1)
    after = shifted(coarse, "gx", -1)
    joined = jnp.concatenate([before, coarse, after], axis=2)
    padded = lax.dynamic_slice_in_dim(joined, planes - 1 - remain, planes + 2, axis=2)

    taps = len(tap_offsets)
    channels = features.shape[1]
    total = jnp.zeros(features.shape, jnp.float32) + conv_bias[None, :, None, None, None]
    for tap_index, (shift_x, shift_y, shift_z) in enumerate(tap_offsets):
        window = jnp.roll(
            padded[:, :, shift_x : shift_x + planes], (1 - shift_y, 1 - shift_z), axis=(3, 4)
        )
        total = total + jnp.einsum(
            "oi,bixyz->boxyz", weight[tap_index], window, preferred_element_type=jnp.float32
        )
    hidden, slope = gelu_parts(total)
    grad_pre = (cotangent.astype(jnp.float32) * slope).astype(jnp.bfloat16)
    grad_before = shifted(grad_pre[:, :, planes - 1 : planes], "gx", 1)
    grad_after = shifted(grad_pre[:, :, 0:1], "gx", -1)
    grad_list = []
    for tap_index, (shift_x, shift_y, shift_z) in enumerate(tap_offsets):
        window = jnp.roll(
            padded[:, :, shift_x : shift_x + planes], (1 - shift_y, 1 - shift_z), axis=(3, 4)
        )
        grad_list.append(
            jnp.einsum("boxyz,bixyz->oi", grad_pre, window, preferred_element_type=jnp.float32)
        )
    grad_b = jnp.sum(grad_pre.astype(jnp.float32), axis=(0, 2, 3, 4))
    stacked = jnp.concatenate([jnp.stack(grad_list).reshape(-1), grad_b])
    summed = butterfly_sum(butterfly_sum(stacked, "dp"), "gx")
    grad_pad = jnp.concatenate([grad_before, grad_pre, grad_after], axis=2)
    grad_in = jnp.zeros(features.shape, jnp.float32)
    for tap_index, (shift_x, shift_y, shift_z) in enumerate(tap_offsets):
        moved_grad = jnp.roll(
            grad_pad[:, :, 2 - shift_x : 2 - shift_x + planes],
            (shift_y - 1, shift_z - 1),
            axis=(3, 4),
        )
        grad_in = grad_in + jnp.einsum(
            "oi,boxyz->bixyz", weight[tap_index], moved_grad, preferred_element_type=jnp.float32
        )
    cell_count = (
        features.shape[0] * lax.axis_size("dp") * length_x * features.shape[3] * features.shape[4]
    )
    grad_scale = 1.0 / math.sqrt(cell_count)
    summed = summed * grad_scale
    weight_count = taps * channels * channels
    return (
        hidden.astype(jnp.bfloat16),
        grad_in.astype(jnp.bfloat16),
        summed[:weight_count].reshape(taps, channels, channels),
        summed[weight_count:],
    )


def solution(mesh):
    in_specs = (
        P("dp", None, "gx", None, None),
        P("dp", None),
        P("dp", None),
        P(),
        P(),
        P("dp", None, "gx", None, None),
    )
    out_specs = (P("dp", None, "gx", None, None), P("dp", None, "gx", None, None), P(), P())
    return jax.shard_map(
        on_device, mesh=mesh, in_specs=in_specs, out_specs=out_specs, check_vma=False
    )
```

```python
import math

import jax
import jax.numpy as jnp
from jax import lax
from jax.sharding import PartitionSpec as P

tap_offsets = [
    (shift_x, shift_y, shift_z)
    for shift_x in range(3)
    for shift_y in range(3)
    for shift_z in range(3)
]


def shifted(value, axis, steps):
    count = lax.axis_size(axis)
    pairs = [(source, (source + steps) % count) for source in range(count)]
    return lax.ppermute(value, axis, pairs)


def butterfly_sum(value, axis):
    count = lax.axis_size(axis)
    here = lax.axis_index(axis)
    step = 1
    while step < count:
        if step * 4 <= count:
            found = [value] + [
                lax.ppermute(value, axis, [(peer, peer ^ (m * step)) for peer in range(count)])
                for m in (1, 2, 3)
            ]
            stacked = jnp.stack(found)
            place = here // step % 4
            ordered = [stacked[jnp.bitwise_xor(j, place)] for j in range(4)]
            value = (ordered[0] + ordered[1]) + (ordered[2] + ordered[3])
            step *= 4
        else:
            pairs = [(peer, peer ^ step) for peer in range(count)]
            value = value + lax.ppermute(value, axis, pairs)
            step *= 2
    return value


def permute_axis(volume, offset, mirror_bit, dim_index):
    reverse = jnp.flip(volume, dim_index)
    return jnp.where(
        mirror_bit == 1,
        jnp.roll(reverse, -offset, axis=dim_index),
        jnp.roll(volume, offset, axis=dim_index),
    )


def augment_local(volume, offset, mirror_bits):
    volume = permute_axis(volume, offset[1], mirror_bits[1], 2)
    return permute_axis(volume, offset[2], mirror_bits[2], 3)


def gelu_parts(pre_act):
    normal_cdf = 0.5 * (1.0 + lax.erf(pre_act * 0.7071067811865476))
    density = jnp.exp(-0.5 * pre_act * pre_act) * 0.3989422804014327
    return (pre_act * normal_cdf, normal_cdf + pre_act * density)


def routed(pieces, axis, sign, constants):
    count = lax.axis_size(axis)
    here = lax.axis_index(axis)
    step = 1
    while step < count:
        pairs = [(peer, peer ^ step) for peer in range(count)]
        sizes = [piece.shape[2] for piece in pieces]
        arrived = lax.ppermute(jnp.concatenate(pieces, axis=2), axis, pairs)
        updated = []
        begin = 0
        for piece, size, constant in zip(pieces, sizes, constants):
            wanted = jnp.mod(sign * (here - constant), 2 * step)
            take = (wanted // step % 2) != (here // step % 2)
            updated.append(jnp.where(take, arrived[:, :, begin : begin + size], piece))
            begin += size
        pieces = updated
        step *= 2
    return pieces


def on_device(features, offsets, flip_bits, weight, conv_bias, cotangent):
    planes = features.shape[2]
    devices_x = lax.axis_size("gx")
    length_x = planes * devices_x
    local = jax.vmap(augment_local)(features, offsets, flip_bits)
    flip_x = flip_bits[0, 0] == 1
    block = jnp.where(flip_x, jnp.flip(local, 2), local)
    effective = jnp.where(flip_x, jnp.mod(-offsets[0, 0], length_x), offsets[0, 0])
    coarse_steps = effective // planes
    remain = effective % planes
    sign = jnp.where(flip_x, -1, 1)
    constant = jnp.where(flip_x, devices_x - 1 + coarse_steps, coarse_steps)
    before, coarse, after = routed(
        [block, block, block[:, :, 0:1]], "gx", sign, [constant + 1, constant, constant - 1]
    )
    joined = jnp.concatenate([before, coarse, after], axis=2)
    padded = lax.dynamic_slice_in_dim(joined, planes - 1 - remain, planes + 2, axis=2)

    taps = len(tap_offsets)
    channels = features.shape[1]
    total = jnp.zeros(features.shape, jnp.float32) + conv_bias[None, :, None, None, None]
    for tap_index, (shift_x, shift_y, shift_z) in enumerate(tap_offsets):
        window = jnp.roll(
            padded[:, :, shift_x : shift_x + planes], (1 - shift_y, 1 - shift_z), axis=(3, 4)
        )
        total = total + jnp.einsum(
            "oi,bixyz->boxyz", weight[tap_index], window, preferred_element_type=jnp.float32
        )
    hidden, slope = gelu_parts(total)
    grad_pre = (cotangent.astype(jnp.float32) * slope).astype(jnp.bfloat16)
    grad_before = shifted(grad_pre[:, :, planes - 1 : planes], "gx", 1)
    grad_after = shifted(grad_pre[:, :, 0:1], "gx", -1)
    grad_list = []
    for tap_index, (shift_x, shift_y, shift_z) in enumerate(tap_offsets):
        window = jnp.roll(
            padded[:, :, shift_x : shift_x + planes], (1 - shift_y, 1 - shift_z), axis=(3, 4)
        )
        grad_list.append(
            jnp.einsum("boxyz,bixyz->oi", grad_pre, window, preferred_element_type=jnp.float32)
        )
    grad_b = jnp.sum(grad_pre.astype(jnp.float32), axis=(0, 2, 3, 4))
    stacked = jnp.concatenate([jnp.stack(grad_list).reshape(-1), grad_b])
    summed = butterfly_sum(butterfly_sum(stacked, "dp"), "gx")
    grad_pad = jnp.concatenate([grad_before, grad_pre, grad_after], axis=2)
    grad_in = jnp.zeros(features.shape, jnp.float32)
    for tap_index, (shift_x, shift_y, shift_z) in enumerate(tap_offsets):
        moved_grad = jnp.roll(
            grad_pad[:, :, 2 - shift_x : 2 - shift_x + planes],
            (shift_y - 1, shift_z - 1),
            axis=(3, 4),
        )
        grad_in = grad_in + jnp.einsum(
            "oi,boxyz->bixyz", weight[tap_index], moved_grad, preferred_element_type=jnp.float32
        )
    cell_count = (
        features.shape[0] * lax.axis_size("dp") * length_x * features.shape[3] * features.shape[4]
    )
    grad_scale = 1.0 / math.sqrt(cell_count)
    summed = summed * grad_scale
    weight_count = taps * channels * channels
    return (
        hidden.astype(jnp.bfloat16),
        grad_in.astype(jnp.bfloat16),
        summed[:weight_count].reshape(taps, channels, channels),
        summed[weight_count:],
    )


def solution(mesh):
    in_specs = (
        P("dp", None, "gx", None, None),
        P("dp", None),
        P("dp", None),
        P(),
        P(),
        P("dp", None, "gx", None, None),
    )
    out_specs = (P("dp", None, "gx", None, None), P("dp", None, "gx", None, None), P(), P())
    return jax.shard_map(
        on_device, mesh=mesh, in_specs=in_specs, out_specs=out_specs, check_vma=False
    )
```

```python
import math

import jax
import jax.numpy as jnp
from jax import lax
from jax.sharding import PartitionSpec as P

tap_offsets = [
    (shift_x, shift_y, shift_z)
    for shift_x in range(3)
    for shift_y in range(3)
    for shift_z in range(3)
]


def shifted(value, axis, steps):
    count = lax.axis_size(axis)
    pairs = [(source, (source + steps) % count) for source in range(count)]
    return lax.ppermute(value, axis, pairs)


def butterfly_sum(value, axis):
    count = lax.axis_size(axis)
    step = 1
    while step < count:
        pairs = [(source, source ^ step) for source in range(count)]
        value = value + lax.ppermute(value, axis, pairs)
        step *= 2
    return value


def permute_axis(volume, offset, mirror_bit, dim_index):
    reverse = jnp.flip(volume, dim_index)
    return jnp.where(
        mirror_bit == 1,
        jnp.roll(reverse, -offset, axis=dim_index),
        jnp.roll(volume, offset, axis=dim_index),
    )


def augment_local(volume, offset, mirror_bits):
    volume = permute_axis(volume, offset[1], mirror_bits[1], 2)
    return permute_axis(volume, offset[2], mirror_bits[2], 3)


def gelu_parts(pre_act):
    normal_cdf = 0.5 * (1.0 + lax.erf(pre_act * 0.7071067811865476))
    density = jnp.exp(-0.5 * pre_act * pre_act) * 0.3989422804014327
    return (pre_act * normal_cdf, normal_cdf + pre_act * density)


def routed(value, axis, sign, constant):
    count = lax.axis_size(axis)
    here = lax.axis_index(axis)
    step = 1
    while step < count:
        low = jnp.mod(sign * (here - constant), step)
        source = here // (2 * step) * (2 * step) + here % (2 * step) // step * step + low
        target = jnp.mod(sign * source + constant, count)
        swap = (source // step % 2) != (target // step % 2)
        pairs = [(peer, peer ^ step) for peer in range(count)]
        value = jnp.where(swap, lax.ppermute(value, axis, pairs), value)
        step *= 2
    return value


def on_device(features, offsets, flip_bits, weight, conv_bias, cotangent):
    planes = features.shape[2]
    devices_x = lax.axis_size("gx")
    length_x = planes * devices_x
    flip_x = flip_bits[0, 0] == 1
    block = jnp.where(flip_x, jnp.flip(features, 2), features)
    effective = jnp.where(flip_x, jnp.mod(-offsets[0, 0], length_x), offsets[0, 0])
    coarse_steps = effective // planes
    remain = effective % planes
    sign = jnp.where(flip_x, -1, 1)
    constant = jnp.where(flip_x, devices_x - 1 + coarse_steps, coarse_steps)
    coarse = routed(block, "gx", sign, constant)
    before = shifted(coarse, "gx", 1)
    after = shifted(coarse[:, :, 0:1], "gx", -1)
    joined = jnp.concatenate([before, coarse, after], axis=2)
    window = lax.dynamic_slice_in_dim(joined, planes - 1 - remain, planes + 2, axis=2)
    padded = jax.vmap(augment_local)(window, offsets, flip_bits)

    taps = len(tap_offsets)
    channels = features.shape[1]
    total = jnp.zeros(features.shape, jnp.float32) + conv_bias[None, :, None, None, None]
    for tap_index, (shift_x, shift_y, shift_z) in enumerate(tap_offsets):
        window = jnp.roll(
            padded[:, :, shift_x : shift_x + planes], (1 - shift_y, 1 - shift_z), axis=(3, 4)
        )
        total = total + jnp.einsum(
            "oi,bixyz->boxyz", weight[tap_index], window, preferred_element_type=jnp.float32
        )
    hidden, slope = gelu_parts(total)
    grad_pre = (cotangent.astype(jnp.float32) * slope).astype(jnp.bfloat16)
    grad_before = shifted(grad_pre[:, :, planes - 1 : planes], "gx", 1)
    grad_after = shifted(grad_pre[:, :, 0:1], "gx", -1)
    grad_list = []
    for tap_index, (shift_x, shift_y, shift_z) in enumerate(tap_offsets):
        window = jnp.roll(
            padded[:, :, shift_x : shift_x + planes], (1 - shift_y, 1 - shift_z), axis=(3, 4)
        )
        grad_list.append(
            jnp.einsum("boxyz,bixyz->oi", grad_pre, window, preferred_element_type=jnp.float32)
        )
    grad_b = jnp.sum(grad_pre.astype(jnp.float32), axis=(0, 2, 3, 4))
    stacked = jnp.concatenate([jnp.stack(grad_list).reshape(-1), grad_b])
    summed = butterfly_sum(butterfly_sum(stacked, "dp"), "gx")
    grad_pad = jnp.concatenate([grad_before, grad_pre, grad_after], axis=2)
    grad_in = jnp.zeros(features.shape, jnp.float32)
    for tap_index, (shift_x, shift_y, shift_z) in enumerate(tap_offsets):
        moved_grad = jnp.roll(
            grad_pad[:, :, 2 - shift_x : 2 - shift_x + planes],
            (shift_y - 1, shift_z - 1),
            axis=(3, 4),
        )
        grad_in = grad_in + jnp.einsum(
            "oi,boxyz->bixyz", weight[tap_index], moved_grad, preferred_element_type=jnp.float32
        )
    cell_count = (
        features.shape[0] * lax.axis_size("dp") * length_x * features.shape[3] * features.shape[4]
    )
    grad_scale = 1.0 / math.sqrt(cell_count)
    summed = summed * grad_scale
    weight_count = taps * channels * channels
    return (
        hidden.astype(jnp.bfloat16),
        grad_in.astype(jnp.bfloat16),
        summed[:weight_count].reshape(taps, channels, channels),
        summed[weight_count:],
    )


def solution(mesh):
    in_specs = (
        P("dp", None, "gx", None, None),
        P("dp", None),
        P("dp", None),
        P(),
        P(),
        P("dp", None, "gx", None, None),
    )
    out_specs = (P("dp", None, "gx", None, None), P("dp", None, "gx", None, None), P(), P())
    return jax.shard_map(
        on_device, mesh=mesh, in_specs=in_specs, out_specs=out_specs, check_vma=False
    )
```

```python
import math

import jax
import jax.numpy as jnp
from jax import lax
from jax.sharding import PartitionSpec as P

tap_offsets = [
    (shift_x, shift_y, shift_z)
    for shift_x in range(3)
    for shift_y in range(3)
    for shift_z in range(3)
]


def shifted(value, axis, steps):
    count = lax.axis_size(axis)
    pairs = [(source, (source + steps) % count) for source in range(count)]
    return lax.ppermute(value, axis, pairs)


def butterfly_sum(value, axis):
    count = lax.axis_size(axis)
    step = 1
    while step < count:
        pairs = [(source, source ^ step) for source in range(count)]
        value = value + lax.ppermute(value, axis, pairs)
        step *= 2
    return value


def permute_axis(volume, offset, mirror_bit, dim_index):
    reverse = jnp.flip(volume, dim_index)
    return jnp.where(
        mirror_bit == 1,
        jnp.roll(reverse, -offset, axis=dim_index),
        jnp.roll(volume, offset, axis=dim_index),
    )


def augment_local(volume, offset, mirror_bits):
    volume = permute_axis(volume, offset[1], mirror_bits[1], 2)
    return permute_axis(volume, offset[2], mirror_bits[2], 3)


def gelu_parts(pre_act):
    normal_cdf = 0.5 * (1.0 + lax.erf(pre_act * 0.7071067811865476))
    density = jnp.exp(-0.5 * pre_act * pre_act) * 0.3989422804014327
    return (pre_act * normal_cdf, normal_cdf + pre_act * density)


def routed(pieces, axis, sign, constants):
    count = lax.axis_size(axis)
    here = lax.axis_index(axis)
    step = 1
    while step < count:
        pairs = [(peer, peer ^ step) for peer in range(count)]
        arrived = lax.ppermute(jnp.concatenate(pieces, axis=2), axis, pairs)
        updated = []
        begin = 0
        for piece, constant in zip(pieces, constants):
            size = piece.shape[2]
            wanted = jnp.mod(sign * (here - constant), 2 * step)
            take = (wanted // step % 2) != (here // step % 2)
            updated.append(jnp.where(take, arrived[:, :, begin : begin + size], piece))
            begin += size
        pieces = updated
        step *= 2
    return pieces


def on_device(features, offsets, flip_bits, weight, conv_bias, cotangent):
    planes = features.shape[2]
    devices_x = lax.axis_size("gx")
    length_x = planes * devices_x
    flip_x = flip_bits[0, 0] == 1
    block = jnp.where(flip_x, jnp.flip(features, 2), features)
    effective = jnp.where(flip_x, jnp.mod(-offsets[0, 0], length_x), offsets[0, 0])
    coarse_steps = effective // planes
    remain = effective % planes
    sign = jnp.where(flip_x, -1, 1)
    constant = jnp.where(flip_x, devices_x - 1 + coarse_steps, coarse_steps)
    if planes == 2:
        coarse, last_before, first_other = routed(
            [block, block[:, :, 1:2], block[:, :, 0:1]],
            "gx",
            sign,
            [constant, constant + 1, jnp.where(remain == 0, constant - 1, constant + 1)],
        )
        window = jnp.where(
            remain == 0,
            jnp.concatenate([last_before, coarse, first_other], axis=2),
            jnp.concatenate([first_other, last_before, coarse], axis=2),
        )
    else:
        (coarse,) = routed([block], "gx", sign, [constant])
        before = shifted(coarse, "gx", 1)
        after = shifted(coarse[:, :, 0:1], "gx", -1)
        joined = jnp.concatenate([before, coarse, after], axis=2)
        window = lax.dynamic_slice_in_dim(joined, planes - 1 - remain, planes + 2, axis=2)
    padded = jax.vmap(augment_local)(window, offsets, flip_bits)

    taps = len(tap_offsets)
    channels = features.shape[1]
    total = jnp.zeros(features.shape, jnp.float32) + conv_bias[None, :, None, None, None]
    for tap_index, (shift_x, shift_y, shift_z) in enumerate(tap_offsets):
        window = jnp.roll(
            padded[:, :, shift_x : shift_x + planes], (1 - shift_y, 1 - shift_z), axis=(3, 4)
        )
        total = total + jnp.einsum(
            "oi,bixyz->boxyz", weight[tap_index], window, preferred_element_type=jnp.float32
        )
    hidden, slope = gelu_parts(total)
    grad_pre = (cotangent.astype(jnp.float32) * slope).astype(jnp.bfloat16)
    grad_before = shifted(grad_pre[:, :, planes - 1 : planes], "gx", 1)
    grad_after = shifted(grad_pre[:, :, 0:1], "gx", -1)
    grad_list = []
    for tap_index, (shift_x, shift_y, shift_z) in enumerate(tap_offsets):
        window = jnp.roll(
            padded[:, :, shift_x : shift_x + planes], (1 - shift_y, 1 - shift_z), axis=(3, 4)
        )
        grad_list.append(
            jnp.einsum("boxyz,bixyz->oi", grad_pre, window, preferred_element_type=jnp.float32)
        )
    grad_b = jnp.sum(grad_pre.astype(jnp.float32), axis=(0, 2, 3, 4))
    stacked = jnp.concatenate([jnp.stack(grad_list).reshape(-1), grad_b])
    summed = butterfly_sum(butterfly_sum(stacked, "dp"), "gx")
    grad_pad = jnp.concatenate([grad_before, grad_pre, grad_after], axis=2)
    grad_in = jnp.zeros(features.shape, jnp.float32)
    for tap_index, (shift_x, shift_y, shift_z) in enumerate(tap_offsets):
        moved_grad = jnp.roll(
            grad_pad[:, :, 2 - shift_x : 2 - shift_x + planes],
            (shift_y - 1, shift_z - 1),
            axis=(3, 4),
        )
        grad_in = grad_in + jnp.einsum(
            "oi,boxyz->bixyz", weight[tap_index], moved_grad, preferred_element_type=jnp.float32
        )
    cell_count = (
        features.shape[0] * lax.axis_size("dp") * length_x * features.shape[3] * features.shape[4]
    )
    grad_scale = 1.0 / math.sqrt(cell_count)
    summed = summed * grad_scale
    weight_count = taps * channels * channels
    return (
        hidden.astype(jnp.bfloat16),
        grad_in.astype(jnp.bfloat16),
        summed[:weight_count].reshape(taps, channels, channels),
        summed[weight_count:],
    )


def solution(mesh):
    in_specs = (
        P("dp", None, "gx", None, None),
        P("dp", None),
        P("dp", None),
        P(),
        P(),
        P("dp", None, "gx", None, None),
    )
    out_specs = (P("dp", None, "gx", None, None), P("dp", None, "gx", None, None), P(), P())
    return jax.shard_map(
        on_device, mesh=mesh, in_specs=in_specs, out_specs=out_specs, check_vma=False
    )
```

```python
import math

import jax
import jax.numpy as jnp
from jax import lax
from jax.sharding import PartitionSpec as P

tap_offsets = [
    (shift_x, shift_y, shift_z)
    for shift_x in range(3)
    for shift_y in range(3)
    for shift_z in range(3)
]


def shifted(value, axis, steps):
    count = lax.axis_size(axis)
    pairs = [(source, (source + steps) % count) for source in range(count)]
    return lax.ppermute(value, axis, pairs)


def butterfly_sum(value, axis):
    count = lax.axis_size(axis)
    step = 1
    while step < count:
        pairs = [(source, source ^ step) for source in range(count)]
        value = value + lax.ppermute(value, axis, pairs)
        step *= 2
    return value


def permute_axis(volume, offset, mirror_bit, dim_index):
    reverse = jnp.flip(volume, dim_index)
    return jnp.where(
        mirror_bit == 1,
        jnp.roll(reverse, -offset, axis=dim_index),
        jnp.roll(volume, offset, axis=dim_index),
    )


def augment_local(volume, offset, mirror_bits):
    volume = permute_axis(volume, offset[1], mirror_bits[1], 2)
    return permute_axis(volume, offset[2], mirror_bits[2], 3)


def gelu_parts(pre_act):
    normal_cdf = 0.5 * (1.0 + lax.erf(pre_act * 0.7071067811865476))
    density = jnp.exp(-0.5 * pre_act * pre_act) * 0.3989422804014327
    return (pre_act * normal_cdf, normal_cdf + pre_act * density)


def routed(pieces, axis, sign, constants):
    count = lax.axis_size(axis)
    here = lax.axis_index(axis)
    step = 1
    while step < count:
        pairs = [(peer, peer ^ step) for peer in range(count)]
        arrived = lax.ppermute(jnp.concatenate(pieces, axis=2), axis, pairs)
        updated = []
        begin = 0
        for piece, constant in zip(pieces, constants):
            size = piece.shape[2]
            wanted = jnp.mod(sign * (here - constant), 2 * step)
            take = (wanted // step % 2) != (here // step % 2)
            updated.append(jnp.where(take, arrived[:, :, begin : begin + size], piece))
            begin += size
        pieces = updated
        step *= 2
    return pieces


def on_device(features, offsets, flip_bits, weight, conv_bias, cotangent):
    planes = features.shape[2]
    devices_x = lax.axis_size("gx")
    length_x = planes * devices_x
    flip_x = flip_bits[0, 0] == 1
    block = jnp.where(flip_x, jnp.flip(features, 2), features)
    effective = jnp.where(flip_x, jnp.mod(-offsets[0, 0], length_x), offsets[0, 0])
    coarse_steps = effective // planes
    remain = effective % planes
    sign = jnp.where(flip_x, -1, 1)
    constant = jnp.where(flip_x, devices_x - 1 + coarse_steps, coarse_steps)
    if planes == 2:
        coarse, last_before, first_other = routed(
            [block, block[:, :, 1:2], block[:, :, 0:1]],
            "gx",
            sign,
            [constant, constant + 1, jnp.where(remain == 0, constant - 1, constant + 1)],
        )
        window = jnp.where(
            remain == 0,
            jnp.concatenate([last_before, coarse, first_other], axis=2),
            jnp.concatenate([first_other, last_before, coarse], axis=2),
        )
    else:
        (coarse,) = routed([block], "gx", sign, [constant])
        before = shifted(coarse, "gx", 1)
        after = shifted(coarse[:, :, 0:1], "gx", -1)
        joined = jnp.concatenate([before, coarse, after], axis=2)
        window = lax.dynamic_slice_in_dim(joined, planes - 1 - remain, planes + 2, axis=2)
    padded = jax.vmap(augment_local)(window, offsets, flip_bits)

    taps = len(tap_offsets)
    channels = features.shape[1]
    kernel = weight.reshape(3, 3, 3, channels, channels)
    stacked_z = jnp.concatenate([jnp.roll(padded, 1 - h, axis=4) for h in range(3)], axis=1)
    total = jnp.zeros(features.shape, jnp.float32) + conv_bias[None, :, None, None, None]
    for shift_x in range(3):
        for shift_y in range(3):
            window = jnp.roll(stacked_z[:, :, shift_x : shift_x + planes], 1 - shift_y, axis=3)
            mixed = jnp.transpose(kernel[shift_x, shift_y], (1, 0, 2)).reshape(channels, -1)
            total = total + jnp.einsum(
                "oc,bcxyz->boxyz", mixed, window, preferred_element_type=jnp.float32
            )
    hidden, slope = gelu_parts(total)
    grad_pre = (cotangent.astype(jnp.float32) * slope).astype(jnp.bfloat16)
    grad_before = shifted(grad_pre[:, :, planes - 1 : planes], "gx", 1)
    grad_after = shifted(grad_pre[:, :, 0:1], "gx", -1)
    grad_list = []
    for shift_x in range(3):
        for shift_y in range(3):
            window = jnp.roll(stacked_z[:, :, shift_x : shift_x + planes], 1 - shift_y, axis=3)
            part = jnp.einsum(
                "boxyz,bcxyz->oc", grad_pre, window, preferred_element_type=jnp.float32
            )
            grad_list.append(jnp.transpose(part.reshape(channels, 3, channels), (1, 0, 2)))
    grad_b = jnp.sum(grad_pre.astype(jnp.float32), axis=(0, 2, 3, 4))
    stacked = jnp.concatenate([jnp.concatenate(grad_list, axis=0).reshape(-1), grad_b])
    summed = butterfly_sum(butterfly_sum(stacked, "dp"), "gx")
    grad_pad = jnp.concatenate([grad_before, grad_pre, grad_after], axis=2)
    grad_z = jnp.concatenate([jnp.roll(grad_pad, h - 1, axis=4) for h in range(3)], axis=1)
    grad_in = jnp.zeros(features.shape, jnp.float32)
    for shift_x in range(3):
        for shift_y in range(3):
            moved_grad = jnp.roll(
                grad_z[:, :, 2 - shift_x : 2 - shift_x + planes], shift_y - 1, axis=3
            )
            mixed = kernel[shift_x, shift_y].reshape(-1, channels)
            grad_in = grad_in + jnp.einsum(
                "ci,bcxyz->bixyz", mixed, moved_grad, preferred_element_type=jnp.float32
            )
    cell_count = (
        features.shape[0] * lax.axis_size("dp") * length_x * features.shape[3] * features.shape[4]
    )
    grad_scale = 1.0 / math.sqrt(cell_count)
    summed = summed * grad_scale
    weight_count = taps * channels * channels
    return (
        hidden.astype(jnp.bfloat16),
        grad_in.astype(jnp.bfloat16),
        summed[:weight_count].reshape(taps, channels, channels),
        summed[weight_count:],
    )


def solution(mesh):
    in_specs = (
        P("dp", None, "gx", None, None),
        P("dp", None),
        P("dp", None),
        P(),
        P(),
        P("dp", None, "gx", None, None),
    )
    out_specs = (P("dp", None, "gx", None, None), P("dp", None, "gx", None, None), P(), P())
    return jax.shard_map(
        on_device, mesh=mesh, in_specs=in_specs, out_specs=out_specs, check_vma=False
    )
```

```python
import math

import jax
import jax.numpy as jnp
from jax import lax
from jax.sharding import PartitionSpec as P

tap_offsets = [
    (shift_x, shift_y, shift_z)
    for shift_x in range(3)
    for shift_y in range(3)
    for shift_z in range(3)
]


def shifted(value, axis, steps):
    count = lax.axis_size(axis)
    pairs = [(source, (source + steps) % count) for source in range(count)]
    return lax.ppermute(value, axis, pairs)


def butterfly_sum(value, axis):
    count = lax.axis_size(axis)
    step = 1
    while step < count:
        pairs = [(source, source ^ step) for source in range(count)]
        value = value + lax.ppermute(value, axis, pairs)
        step *= 2
    return value


def permute_axis(volume, offset, mirror_bit, dim_index):
    reverse = jnp.flip(volume, dim_index)
    return jnp.where(
        mirror_bit == 1,
        jnp.roll(reverse, -offset, axis=dim_index),
        jnp.roll(volume, offset, axis=dim_index),
    )


def augment_local(volume, offset, mirror_bits):
    volume = permute_axis(volume, offset[1], mirror_bits[1], 2)
    return permute_axis(volume, offset[2], mirror_bits[2], 3)


def gelu_parts(pre_act):
    normal_cdf = 0.5 * (1.0 + lax.erf(pre_act * 0.7071067811865476))
    density = jnp.exp(-0.5 * pre_act * pre_act) * 0.3989422804014327
    return (pre_act * normal_cdf, normal_cdf + pre_act * density)


def routed(pieces, axis, sign, constants):
    count = lax.axis_size(axis)
    here = lax.axis_index(axis)
    step = count // 2
    while step >= 1:
        pairs = [(peer, peer ^ step) for peer in range(count)]
        arrived = lax.ppermute(jnp.concatenate(pieces, axis=2), axis, pairs)
        updated = []
        begin = 0
        for piece, constant in zip(pieces, constants):
            size = piece.shape[2]
            landed = jnp.mod(sign * (here % step) + constant, count)
            rest = jnp.mod(sign * (here // step - landed // step), count // step)
            take = (rest % 2) != (here // step % 2)
            updated.append(jnp.where(take, arrived[:, :, begin : begin + size], piece))
            begin += size
        pieces = updated
        step //= 2
    return pieces


def on_device(features, offsets, flip_bits, weight, conv_bias, cotangent):
    planes = features.shape[2]
    devices_x = lax.axis_size("gx")
    length_x = planes * devices_x
    flip_x = flip_bits[0, 0] == 1
    block = jnp.where(flip_x, jnp.flip(features, 2), features)
    effective = jnp.where(flip_x, jnp.mod(-offsets[0, 0], length_x), offsets[0, 0])
    coarse_steps = effective // planes
    remain = effective % planes
    sign = jnp.where(flip_x, -1, 1)
    constant = jnp.where(flip_x, devices_x - 1 + coarse_steps, coarse_steps)
    if planes == 2:
        coarse, last_before, first_other = routed(
            [block, block[:, :, 1:2], block[:, :, 0:1]],
            "gx",
            sign,
            [constant, constant + 1, jnp.where(remain == 0, constant - 1, constant + 1)],
        )
        window = jnp.where(
            remain == 0,
            jnp.concatenate([last_before, coarse, first_other], axis=2),
            jnp.concatenate([first_other, last_before, coarse], axis=2),
        )
    else:
        (coarse,) = routed([block], "gx", sign, [constant])
        before = shifted(coarse, "gx", 1)
        after = shifted(coarse[:, :, 0:1], "gx", -1)
        joined = jnp.concatenate([before, coarse, after], axis=2)
        window = lax.dynamic_slice_in_dim(joined, planes - 1 - remain, planes + 2, axis=2)
    padded = jax.vmap(augment_local)(window, offsets, flip_bits)

    taps = len(tap_offsets)
    channels = features.shape[1]
    kernel = weight.reshape(3, 3, 3, channels, channels)
    stacked_z = jnp.concatenate([jnp.roll(padded, 1 - h, axis=4) for h in range(3)], axis=1)
    total = jnp.zeros(features.shape, jnp.float32) + conv_bias[None, :, None, None, None]
    for shift_x in range(3):
        for shift_y in range(3):
            window = jnp.roll(stacked_z[:, :, shift_x : shift_x + planes], 1 - shift_y, axis=3)
            mixed = jnp.transpose(kernel[shift_x, shift_y], (1, 0, 2)).reshape(channels, -1)
            total = total + jnp.einsum(
                "oc,bcxyz->boxyz", mixed, window, preferred_element_type=jnp.float32
            )
    hidden, slope = gelu_parts(total)
    grad_pre = (cotangent.astype(jnp.float32) * slope).astype(jnp.bfloat16)
    grad_before = shifted(grad_pre[:, :, planes - 1 : planes], "gx", 1)
    grad_after = shifted(grad_pre[:, :, 0:1], "gx", -1)
    grad_list = []
    for shift_x in range(3):
        for shift_y in range(3):
            window = jnp.roll(stacked_z[:, :, shift_x : shift_x + planes], 1 - shift_y, axis=3)
            part = jnp.einsum(
                "boxyz,bcxyz->oc", grad_pre, window, preferred_element_type=jnp.float32
            )
            grad_list.append(jnp.transpose(part.reshape(channels, 3, channels), (1, 0, 2)))
    grad_b = jnp.sum(grad_pre.astype(jnp.float32), axis=(0, 2, 3, 4))
    stacked = jnp.concatenate([jnp.concatenate(grad_list, axis=0).reshape(-1), grad_b])
    summed = butterfly_sum(butterfly_sum(stacked, "dp"), "gx")
    grad_pad = jnp.concatenate([grad_before, grad_pre, grad_after], axis=2)
    grad_z = jnp.concatenate([jnp.roll(grad_pad, h - 1, axis=4) for h in range(3)], axis=1)
    grad_in = jnp.zeros(features.shape, jnp.float32)
    for shift_x in range(3):
        for shift_y in range(3):
            moved_grad = jnp.roll(
                grad_z[:, :, 2 - shift_x : 2 - shift_x + planes], shift_y - 1, axis=3
            )
            mixed = kernel[shift_x, shift_y].reshape(-1, channels)
            grad_in = grad_in + jnp.einsum(
                "ci,bcxyz->bixyz", mixed, moved_grad, preferred_element_type=jnp.float32
            )
    cell_count = (
        features.shape[0] * lax.axis_size("dp") * length_x * features.shape[3] * features.shape[4]
    )
    grad_scale = 1.0 / math.sqrt(cell_count)
    summed = summed * grad_scale
    weight_count = taps * channels * channels
    return (
        hidden.astype(jnp.bfloat16),
        grad_in.astype(jnp.bfloat16),
        summed[:weight_count].reshape(taps, channels, channels),
        summed[weight_count:],
    )


def solution(mesh):
    in_specs = (
        P("dp", None, "gx", None, None),
        P("dp", None),
        P("dp", None),
        P(),
        P(),
        P("dp", None, "gx", None, None),
    )
    out_specs = (P("dp", None, "gx", None, None), P("dp", None, "gx", None, None), P(), P())
    return jax.shard_map(
        on_device, mesh=mesh, in_specs=in_specs, out_specs=out_specs, check_vma=False
    )
```

```python
import math

import jax
import jax.numpy as jnp
from jax import lax
from jax.sharding import PartitionSpec as P

tap_offsets = [
    (shift_x, shift_y, shift_z)
    for shift_x in range(3)
    for shift_y in range(3)
    for shift_z in range(3)
]


def shifted(value, axis, steps):
    count = lax.axis_size(axis)
    pairs = [(source, (source + steps) % count) for source in range(count)]
    return lax.ppermute(value, axis, pairs)


def butterfly_sum(value, axis):
    count = lax.axis_size(axis)
    step = 1
    while step < count:
        pairs = [(source, source ^ step) for source in range(count)]
        value = value + lax.ppermute(value, axis, pairs)
        step *= 2
    return value


def permute_axis(volume, offset, mirror_bit, dim_index):
    reverse = jnp.flip(volume, dim_index)
    return jnp.where(
        mirror_bit == 1,
        jnp.roll(reverse, -offset, axis=dim_index),
        jnp.roll(volume, offset, axis=dim_index),
    )


def augment_local(volume, offset, mirror_bits):
    volume = permute_axis(volume, offset[1], mirror_bits[1], 2)
    return permute_axis(volume, offset[2], mirror_bits[2], 3)


def gelu_parts(pre_act):
    normal_cdf = 0.5 * (1.0 + lax.erf(pre_act * 0.7071067811865476))
    density = jnp.exp(-0.5 * pre_act * pre_act) * 0.3989422804014327
    return (pre_act * normal_cdf, normal_cdf + pre_act * density)


def routed(pieces, axis, sign, constants):
    count = lax.axis_size(axis)
    here = lax.axis_index(axis)
    step = 1
    while step < count:
        pairs = [(peer, peer ^ step) for peer in range(count)]
        arrived = lax.ppermute(jnp.concatenate(pieces, axis=2), axis, pairs)
        updated = []
        begin = 0
        for piece, constant in zip(pieces, constants):
            size = piece.shape[2]
            wanted = jnp.mod(sign * (here - constant), 2 * step)
            take = (wanted // step % 2) != (here // step % 2)
            updated.append(jnp.where(take, arrived[:, :, begin : begin + size], piece))
            begin += size
        pieces = updated
        step *= 2
    return pieces


def on_device(features, offsets, flip_bits, weight, conv_bias, cotangent):
    planes = features.shape[2]
    devices_x = lax.axis_size("gx")
    length_x = planes * devices_x
    flip_x = flip_bits[0, 0] == 1
    block = jnp.where(flip_x, jnp.flip(features, 2), features)
    effective = jnp.where(flip_x, jnp.mod(-offsets[0, 0], length_x), offsets[0, 0])
    coarse_steps = effective // planes
    remain = effective % planes
    sign = jnp.where(flip_x, -1, 1)
    constant = jnp.where(flip_x, devices_x - 1 + coarse_steps, coarse_steps)
    if planes == 2:
        coarse, last_before, first_other = routed(
            [block, block[:, :, 1:2], block[:, :, 0:1]],
            "gx",
            sign,
            [constant, constant + 1, jnp.where(remain == 0, constant - 1, constant + 1)],
        )
        window = jnp.where(
            remain == 0,
            jnp.concatenate([last_before, coarse, first_other], axis=2),
            jnp.concatenate([first_other, last_before, coarse], axis=2),
        )
    else:
        (coarse,) = routed([block], "gx", sign, [constant])
        before = shifted(coarse, "gx", 1)
        after = shifted(coarse[:, :, 0:1], "gx", -1)
        joined = jnp.concatenate([before, coarse, after], axis=2)
        window = lax.dynamic_slice_in_dim(joined, planes - 1 - remain, planes + 2, axis=2)
    padded = jax.vmap(augment_local)(window, offsets, flip_bits)

    taps = len(tap_offsets)
    channels = features.shape[1]
    kernel = weight.reshape(3, 3, 3, channels, channels)
    rolled = [(1 - e, 1 - h) for e in range(3) for h in range(3)]
    stacked_yz = jnp.concatenate([jnp.roll(padded, r, axis=(3, 4)) for r in rolled], axis=1)
    total = jnp.zeros(features.shape, jnp.float32) + conv_bias[None, :, None, None, None]
    for shift_x in range(3):
        window = stacked_yz[:, :, shift_x : shift_x + planes]
        mixed = jnp.transpose(kernel[shift_x], (2, 0, 1, 3)).reshape(channels, -1)
        total = total + jnp.einsum(
            "oc,bcxyz->boxyz", mixed, window, preferred_element_type=jnp.float32
        )
    hidden, slope = gelu_parts(total)
    grad_pre = (cotangent.astype(jnp.float32) * slope).astype(jnp.bfloat16)
    grad_before = shifted(grad_pre[:, :, planes - 1 : planes], "gx", 1)
    grad_after = shifted(grad_pre[:, :, 0:1], "gx", -1)
    grad_list = []
    for shift_x in range(3):
        window = stacked_yz[:, :, shift_x : shift_x + planes]
        part = jnp.einsum("boxyz,bcxyz->oc", grad_pre, window, preferred_element_type=jnp.float32)
        part = jnp.transpose(part.reshape(channels, 3, 3, channels), (1, 2, 0, 3))
        grad_list.append(part.reshape(9, channels, channels))
    grad_b = jnp.sum(grad_pre.astype(jnp.float32), axis=(0, 2, 3, 4))
    stacked = jnp.concatenate([jnp.concatenate(grad_list, axis=0).reshape(-1), grad_b])
    summed = butterfly_sum(butterfly_sum(stacked, "dp"), "gx")
    grad_pad = jnp.concatenate([grad_before, grad_pre, grad_after], axis=2)
    rolled_back = [(e - 1, h - 1) for e in range(3) for h in range(3)]
    grad_yz = jnp.concatenate([jnp.roll(grad_pad, r, axis=(3, 4)) for r in rolled_back], axis=1)
    grad_in = jnp.zeros(features.shape, jnp.float32)
    for shift_x in range(3):
        moved_grad = grad_yz[:, :, 2 - shift_x : 2 - shift_x + planes]
        mixed = kernel[shift_x].reshape(-1, channels)
        grad_in = grad_in + jnp.einsum(
            "ci,bcxyz->bixyz", mixed, moved_grad, preferred_element_type=jnp.float32
        )
    cell_count = (
        features.shape[0] * lax.axis_size("dp") * length_x * features.shape[3] * features.shape[4]
    )
    grad_scale = 1.0 / math.sqrt(cell_count)
    summed = summed * grad_scale
    weight_count = taps * channels * channels
    return (
        hidden.astype(jnp.bfloat16),
        grad_in.astype(jnp.bfloat16),
        summed[:weight_count].reshape(taps, channels, channels),
        summed[weight_count:],
    )


def solution(mesh):
    in_specs = (
        P("dp", None, "gx", None, None),
        P("dp", None),
        P("dp", None),
        P(),
        P(),
        P("dp", None, "gx", None, None),
    )
    out_specs = (P("dp", None, "gx", None, None), P("dp", None, "gx", None, None), P(), P())
    return jax.shard_map(
        on_device, mesh=mesh, in_specs=in_specs, out_specs=out_specs, check_vma=False
    )
```

```python
import math

import jax
import jax.numpy as jnp
from jax import lax
from jax.sharding import PartitionSpec as P

tap_offsets = [
    (shift_x, shift_y, shift_z)
    for shift_x in range(3)
    for shift_y in range(3)
    for shift_z in range(3)
]


def shifted(value, axis, steps):
    count = lax.axis_size(axis)
    pairs = [(source, (source + steps) % count) for source in range(count)]
    return lax.ppermute(value, axis, pairs)


def butterfly_sum(value, axis):
    count = lax.axis_size(axis)
    step = count // 2
    while step >= 1:
        pairs = [(source, source ^ step) for source in range(count)]
        value = value + lax.ppermute(value, axis, pairs)
        step //= 2
    return value


def permute_axis(volume, offset, mirror_bit, dim_index):
    reverse = jnp.flip(volume, dim_index)
    return jnp.where(
        mirror_bit == 1,
        jnp.roll(reverse, -offset, axis=dim_index),
        jnp.roll(volume, offset, axis=dim_index),
    )


def augment_local(volume, offset, mirror_bits):
    volume = permute_axis(volume, offset[1], mirror_bits[1], 2)
    return permute_axis(volume, offset[2], mirror_bits[2], 3)


def gelu_parts(pre_act):
    normal_cdf = 0.5 * (1.0 + lax.erf(pre_act * 0.7071067811865476))
    density = jnp.exp(-0.5 * pre_act * pre_act) * 0.3989422804014327
    return (pre_act * normal_cdf, normal_cdf + pre_act * density)


def routed(pieces, axis, sign, constants):
    count = lax.axis_size(axis)
    here = lax.axis_index(axis)
    step = 1
    while step < count:
        pairs = [(peer, peer ^ step) for peer in range(count)]
        arrived = lax.ppermute(jnp.concatenate(pieces, axis=2), axis, pairs)
        updated = []
        begin = 0
        for piece, constant in zip(pieces, constants):
            size = piece.shape[2]
            wanted = jnp.mod(sign * (here - constant), 2 * step)
            take = (wanted // step % 2) != (here // step % 2)
            updated.append(jnp.where(take, arrived[:, :, begin : begin + size], piece))
            begin += size
        pieces = updated
        step *= 2
    return pieces


def on_device(features, offsets, flip_bits, weight, conv_bias, cotangent):
    planes = features.shape[2]
    devices_x = lax.axis_size("gx")
    length_x = planes * devices_x
    flip_x = flip_bits[0, 0] == 1
    block = jnp.where(flip_x, jnp.flip(features, 2), features)
    effective = jnp.where(flip_x, jnp.mod(-offsets[0, 0], length_x), offsets[0, 0])
    coarse_steps = effective // planes
    remain = effective % planes
    sign = jnp.where(flip_x, -1, 1)
    constant = jnp.where(flip_x, devices_x - 1 + coarse_steps, coarse_steps)
    if planes == 2:
        coarse, last_before, first_other = routed(
            [block, block[:, :, 1:2], block[:, :, 0:1]],
            "gx",
            sign,
            [constant, constant + 1, jnp.where(remain == 0, constant - 1, constant + 1)],
        )
        window = jnp.where(
            remain == 0,
            jnp.concatenate([last_before, coarse, first_other], axis=2),
            jnp.concatenate([first_other, last_before, coarse], axis=2),
        )
    else:
        (coarse,) = routed([block], "gx", sign, [constant])
        before = shifted(coarse, "gx", 1)
        after = shifted(coarse[:, :, 0:1], "gx", -1)
        joined = jnp.concatenate([before, coarse, after], axis=2)
        window = lax.dynamic_slice_in_dim(joined, planes - 1 - remain, planes + 2, axis=2)
    padded = jax.vmap(augment_local)(window, offsets, flip_bits)

    taps = len(tap_offsets)
    channels = features.shape[1]
    kernel = weight.reshape(3, 3, 3, channels, channels)
    rolled = [(1 - e, 1 - h) for e in range(3) for h in range(3)]
    stacked_yz = jnp.concatenate([jnp.roll(padded, r, axis=(3, 4)) for r in rolled], axis=1)
    total = jnp.zeros(features.shape, jnp.float32) + conv_bias[None, :, None, None, None]
    for shift_x in range(3):
        window = stacked_yz[:, :, shift_x : shift_x + planes]
        mixed = jnp.transpose(kernel[shift_x], (2, 0, 1, 3)).reshape(channels, -1)
        total = total + jnp.einsum(
            "oc,bcxyz->boxyz", mixed, window, preferred_element_type=jnp.float32
        )
    hidden, slope = gelu_parts(total)
    grad_pre = (cotangent.astype(jnp.float32) * slope).astype(jnp.bfloat16)
    grad_before = shifted(grad_pre[:, :, planes - 1 : planes], "gx", 1)
    grad_after = shifted(grad_pre[:, :, 0:1], "gx", -1)
    grad_list = []
    for shift_x in range(3):
        window = stacked_yz[:, :, shift_x : shift_x + planes]
        part = jnp.einsum("boxyz,bcxyz->oc", grad_pre, window, preferred_element_type=jnp.float32)
        part = jnp.transpose(part.reshape(channels, 3, 3, channels), (1, 2, 0, 3))
        grad_list.append(part.reshape(9, channels, channels))
    grad_b = jnp.sum(grad_pre.astype(jnp.float32), axis=(0, 2, 3, 4))
    stacked = jnp.concatenate([jnp.concatenate(grad_list, axis=0).reshape(-1), grad_b])
    summed = butterfly_sum(butterfly_sum(stacked, "gx"), "dp")
    grad_pad = jnp.concatenate([grad_before, grad_pre, grad_after], axis=2)
    rolled_back = [(e - 1, h - 1) for e in range(3) for h in range(3)]
    grad_yz = jnp.concatenate([jnp.roll(grad_pad, r, axis=(3, 4)) for r in rolled_back], axis=1)
    grad_in = jnp.zeros(features.shape, jnp.float32)
    for shift_x in range(3):
        moved_grad = grad_yz[:, :, 2 - shift_x : 2 - shift_x + planes]
        mixed = kernel[shift_x].reshape(-1, channels)
        grad_in = grad_in + jnp.einsum(
            "ci,bcxyz->bixyz", mixed, moved_grad, preferred_element_type=jnp.float32
        )
    cell_count = (
        features.shape[0] * lax.axis_size("dp") * length_x * features.shape[3] * features.shape[4]
    )
    grad_scale = 1.0 / math.sqrt(cell_count)
    summed = summed * grad_scale
    weight_count = taps * channels * channels
    return (
        hidden.astype(jnp.bfloat16),
        grad_in.astype(jnp.bfloat16),
        summed[:weight_count].reshape(taps, channels, channels),
        summed[weight_count:],
    )


def solution(mesh):
    in_specs = (
        P("dp", None, "gx", None, None),
        P("dp", None),
        P("dp", None),
        P(),
        P(),
        P("dp", None, "gx", None, None),
    )
    out_specs = (P("dp", None, "gx", None, None), P("dp", None, "gx", None, None), P(), P())
    return jax.shard_map(
        on_device, mesh=mesh, in_specs=in_specs, out_specs=out_specs, check_vma=False
    )
```

```python
import math

import jax
import jax.numpy as jnp
from jax import lax
from jax.sharding import PartitionSpec as P

tap_offsets = [
    (shift_x, shift_y, shift_z)
    for shift_x in range(3)
    for shift_y in range(3)
    for shift_z in range(3)
]


def shifted(value, axis, steps):
    count = lax.axis_size(axis)
    pairs = [(source, (source + steps) % count) for source in range(count)]
    return lax.ppermute(value, axis, pairs)


def halo_planes(value, axis):
    count = lax.axis_size(axis)
    even = lax.axis_index(axis) % 2 == 0
    first, last = value[:, :, 0:1], value[:, :, -1:]
    near = lax.ppermute(jnp.where(even, last, first), axis, [(s, s ^ 1) for s in range(count)])
    pairs = [(s, (s + 1) % count if s % 2 else (s - 1) % count) for s in range(count)]
    across = lax.ppermute(jnp.where(even, first, last), axis, pairs)
    return jnp.where(even, across, near), jnp.where(even, near, across)


def butterfly_sum(value, axis):
    count = lax.axis_size(axis)
    step = count // 2
    while step >= 1:
        pairs = [(source, source ^ step) for source in range(count)]
        value = value + lax.ppermute(value, axis, pairs)
        step //= 2
    return value


def permute_axis(volume, offset, mirror_bit, dim_index):
    reverse = jnp.flip(volume, dim_index)
    return jnp.where(
        mirror_bit == 1,
        jnp.roll(reverse, -offset, axis=dim_index),
        jnp.roll(volume, offset, axis=dim_index),
    )


def augment_local(volume, offset, mirror_bits):
    volume = permute_axis(volume, offset[1], mirror_bits[1], 2)
    return permute_axis(volume, offset[2], mirror_bits[2], 3)


def gelu_parts(pre_act):
    normal_cdf = 0.5 * (1.0 + lax.erf(pre_act * 0.7071067811865476))
    density = jnp.exp(-0.5 * pre_act * pre_act) * 0.3989422804014327
    return (pre_act * normal_cdf, normal_cdf + pre_act * density)


def routed(pieces, axis, sign, constants):
    count = lax.axis_size(axis)
    here = lax.axis_index(axis)
    step = 1
    while step < count:
        pairs = [(peer, peer ^ step) for peer in range(count)]
        arrived = lax.ppermute(jnp.concatenate(pieces, axis=2), axis, pairs)
        updated = []
        begin = 0
        for piece, constant in zip(pieces, constants):
            size = piece.shape[2]
            wanted = jnp.mod(sign * (here - constant), 2 * step)
            take = (wanted // step % 2) != (here // step % 2)
            updated.append(jnp.where(take, arrived[:, :, begin : begin + size], piece))
            begin += size
        pieces = updated
        step *= 2
    return pieces


def on_device(features, offsets, flip_bits, weight, conv_bias, cotangent):
    planes = features.shape[2]
    devices_x = lax.axis_size("gx")
    length_x = planes * devices_x
    flip_x = flip_bits[0, 0] == 1
    block = jnp.where(flip_x, jnp.flip(features, 2), features)
    effective = jnp.where(flip_x, jnp.mod(-offsets[0, 0], length_x), offsets[0, 0])
    coarse_steps = effective // planes
    remain = effective % planes
    sign = jnp.where(flip_x, -1, 1)
    constant = jnp.where(flip_x, devices_x - 1 + coarse_steps, coarse_steps)
    if planes == 2:
        coarse, last_before, first_other = routed(
            [block, block[:, :, 1:2], block[:, :, 0:1]],
            "gx",
            sign,
            [constant, constant + 1, jnp.where(remain == 0, constant - 1, constant + 1)],
        )
        window = jnp.where(
            remain == 0,
            jnp.concatenate([last_before, coarse, first_other], axis=2),
            jnp.concatenate([first_other, last_before, coarse], axis=2),
        )
    else:
        (coarse,) = routed([block], "gx", sign, [constant])
        before = shifted(coarse, "gx", 1)
        after = shifted(coarse[:, :, 0:1], "gx", -1)
        joined = jnp.concatenate([before, coarse, after], axis=2)
        window = lax.dynamic_slice_in_dim(joined, planes - 1 - remain, planes + 2, axis=2)
    padded = jax.vmap(augment_local)(window, offsets, flip_bits)

    taps = len(tap_offsets)
    channels = features.shape[1]
    kernel = weight.reshape(3, 3, 3, channels, channels)
    rolled = [(1 - e, 1 - h) for e in range(3) for h in range(3)]
    stacked_yz = jnp.concatenate([jnp.roll(padded, r, axis=(3, 4)) for r in rolled], axis=1)
    total = jnp.zeros(features.shape, jnp.float32) + conv_bias[None, :, None, None, None]
    for shift_x in range(3):
        window = stacked_yz[:, :, shift_x : shift_x + planes]
        mixed = jnp.transpose(kernel[shift_x], (2, 0, 1, 3)).reshape(channels, -1)
        total = total + jnp.einsum(
            "oc,bcxyz->boxyz", mixed, window, preferred_element_type=jnp.float32
        )
    hidden, slope = gelu_parts(total)
    grad_pre = (cotangent.astype(jnp.float32) * slope).astype(jnp.bfloat16)
    grad_before, grad_after = halo_planes(grad_pre, "gx")
    grad_list = []
    for shift_x in range(3):
        window = stacked_yz[:, :, shift_x : shift_x + planes]
        part = jnp.einsum("boxyz,bcxyz->oc", grad_pre, window, preferred_element_type=jnp.float32)
        part = jnp.transpose(part.reshape(channels, 3, 3, channels), (1, 2, 0, 3))
        grad_list.append(part.reshape(9, channels, channels))
    grad_b = jnp.sum(grad_pre.astype(jnp.float32), axis=(0, 2, 3, 4))
    stacked = jnp.concatenate([jnp.concatenate(grad_list, axis=0).reshape(-1), grad_b])
    summed = butterfly_sum(butterfly_sum(stacked, "gx"), "dp")
    grad_pad = jnp.concatenate([grad_before, grad_pre, grad_after], axis=2)
    rolled_back = [(e - 1, h - 1) for e in range(3) for h in range(3)]
    grad_yz = jnp.concatenate([jnp.roll(grad_pad, r, axis=(3, 4)) for r in rolled_back], axis=1)
    grad_in = jnp.zeros(features.shape, jnp.float32)
    for shift_x in range(3):
        moved_grad = grad_yz[:, :, 2 - shift_x : 2 - shift_x + planes]
        mixed = kernel[shift_x].reshape(-1, channels)
        grad_in = grad_in + jnp.einsum(
            "ci,bcxyz->bixyz", mixed, moved_grad, preferred_element_type=jnp.float32
        )
    cell_count = (
        features.shape[0] * lax.axis_size("dp") * length_x * features.shape[3] * features.shape[4]
    )
    grad_scale = 1.0 / math.sqrt(cell_count)
    summed = summed * grad_scale
    weight_count = taps * channels * channels
    return (
        hidden.astype(jnp.bfloat16),
        grad_in.astype(jnp.bfloat16),
        summed[:weight_count].reshape(taps, channels, channels),
        summed[weight_count:],
    )


def solution(mesh):
    in_specs = (
        P("dp", None, "gx", None, None),
        P("dp", None),
        P("dp", None),
        P(),
        P(),
        P("dp", None, "gx", None, None),
    )
    out_specs = (P("dp", None, "gx", None, None), P("dp", None, "gx", None, None), P(), P())
    return jax.shard_map(
        on_device, mesh=mesh, in_specs=in_specs, out_specs=out_specs, check_vma=False
    )
```

```python
import math

import jax
import jax.numpy as jnp
from jax import lax
from jax.sharding import PartitionSpec as P

tap_offsets = [
    (shift_x, shift_y, shift_z)
    for shift_x in range(3)
    for shift_y in range(3)
    for shift_z in range(3)
]


def shifted(value, axis, steps):
    count = lax.axis_size(axis)
    pairs = [(source, (source + steps) % count) for source in range(count)]
    return lax.ppermute(value, axis, pairs)


def neighbour_blocks(value, axis):
    count = lax.axis_size(axis)
    even = lax.axis_index(axis) % 2 == 0
    near = lax.ppermute(value, axis, [(s, s ^ 1) for s in range(count)])
    pairs = [(s, (s + 1) % count if s % 2 else (s - 1) % count) for s in range(count)]
    across = lax.ppermute(value, axis, pairs)
    return jnp.where(even, across, near), jnp.where(even, near, across)


def halo_planes(value, axis):
    count = lax.axis_size(axis)
    even = lax.axis_index(axis) % 2 == 0
    first, last = value[:, :, 0:1], value[:, :, -1:]
    near = lax.ppermute(jnp.where(even, last, first), axis, [(s, s ^ 1) for s in range(count)])
    pairs = [(s, (s + 1) % count if s % 2 else (s - 1) % count) for s in range(count)]
    across = lax.ppermute(jnp.where(even, first, last), axis, pairs)
    return jnp.where(even, across, near), jnp.where(even, near, across)


def butterfly_sum(value, axis):
    count = lax.axis_size(axis)
    step = count // 2
    while step >= 1:
        pairs = [(source, source ^ step) for source in range(count)]
        value = value + lax.ppermute(value, axis, pairs)
        step //= 2
    return value


def permute_axis(volume, offset, mirror_bit, dim_index):
    reverse = jnp.flip(volume, dim_index)
    return jnp.where(
        mirror_bit == 1,
        jnp.roll(reverse, -offset, axis=dim_index),
        jnp.roll(volume, offset, axis=dim_index),
    )


def augment_local(volume, offset, mirror_bits):
    volume = permute_axis(volume, offset[1], mirror_bits[1], 2)
    return permute_axis(volume, offset[2], mirror_bits[2], 3)


def gelu_parts(pre_act):
    normal_cdf = 0.5 * (1.0 + lax.erf(pre_act * 0.7071067811865476))
    density = jnp.exp(-0.5 * pre_act * pre_act) * 0.3989422804014327
    return (pre_act * normal_cdf, normal_cdf + pre_act * density)


def routed(pieces, axis, sign, constants):
    count = lax.axis_size(axis)
    here = lax.axis_index(axis)
    step = 1
    while step < count:
        pairs = [(peer, peer ^ step) for peer in range(count)]
        arrived = lax.ppermute(jnp.concatenate(pieces, axis=2), axis, pairs)
        updated = []
        begin = 0
        for piece, constant in zip(pieces, constants):
            size = piece.shape[2]
            wanted = jnp.mod(sign * (here - constant), 2 * step)
            take = (wanted // step % 2) != (here // step % 2)
            updated.append(jnp.where(take, arrived[:, :, begin : begin + size], piece))
            begin += size
        pieces = updated
        step *= 2
    return pieces


def on_device(features, offsets, flip_bits, weight, conv_bias, cotangent):
    planes = features.shape[2]
    devices_x = lax.axis_size("gx")
    length_x = planes * devices_x
    flip_x = flip_bits[0, 0] == 1
    block = jnp.where(flip_x, jnp.flip(features, 2), features)
    effective = jnp.where(flip_x, jnp.mod(-offsets[0, 0], length_x), offsets[0, 0])
    coarse_steps = effective // planes
    remain = effective % planes
    sign = jnp.where(flip_x, -1, 1)
    constant = jnp.where(flip_x, devices_x - 1 + coarse_steps, coarse_steps)
    (coarse,) = routed([block], "gx", sign, [constant])
    before, after = neighbour_blocks(coarse, "gx")
    joined = jnp.concatenate([before, coarse, after[:, :, 0:1]], axis=2)
    window = lax.dynamic_slice_in_dim(joined, planes - 1 - remain, planes + 2, axis=2)
    padded = jax.vmap(augment_local)(window, offsets, flip_bits)

    taps = len(tap_offsets)
    channels = features.shape[1]
    kernel = weight.reshape(3, 3, 3, channels, channels)
    rolled = [(1 - e, 1 - h) for e in range(3) for h in range(3)]
    stacked_yz = jnp.concatenate([jnp.roll(padded, r, axis=(3, 4)) for r in rolled], axis=1)
    total = jnp.zeros(features.shape, jnp.float32) + conv_bias[None, :, None, None, None]
    for shift_x in range(3):
        window = stacked_yz[:, :, shift_x : shift_x + planes]
        mixed = jnp.transpose(kernel[shift_x], (2, 0, 1, 3)).reshape(channels, -1)
        total = total + jnp.einsum(
            "oc,bcxyz->boxyz", mixed, window, preferred_element_type=jnp.float32
        )
    hidden, slope = gelu_parts(total)
    grad_pre = (cotangent.astype(jnp.float32) * slope).astype(jnp.bfloat16)
    grad_before, grad_after = halo_planes(grad_pre, "gx")
    grad_list = []
    for shift_x in range(3):
        window = stacked_yz[:, :, shift_x : shift_x + planes]
        part = jnp.einsum("boxyz,bcxyz->oc", grad_pre, window, preferred_element_type=jnp.float32)
        part = jnp.transpose(part.reshape(channels, 3, 3, channels), (1, 2, 0, 3))
        grad_list.append(part.reshape(9, channels, channels))
    grad_b = jnp.sum(grad_pre.astype(jnp.float32), axis=(0, 2, 3, 4))
    stacked = jnp.concatenate([jnp.concatenate(grad_list, axis=0).reshape(-1), grad_b])
    summed = butterfly_sum(butterfly_sum(stacked, "gx"), "dp")
    grad_pad = jnp.concatenate([grad_before, grad_pre, grad_after], axis=2)
    rolled_back = [(e - 1, h - 1) for e in range(3) for h in range(3)]
    grad_yz = jnp.concatenate([jnp.roll(grad_pad, r, axis=(3, 4)) for r in rolled_back], axis=1)
    grad_in = jnp.zeros(features.shape, jnp.float32)
    for shift_x in range(3):
        moved_grad = grad_yz[:, :, 2 - shift_x : 2 - shift_x + planes]
        mixed = kernel[shift_x].reshape(-1, channels)
        grad_in = grad_in + jnp.einsum(
            "ci,bcxyz->bixyz", mixed, moved_grad, preferred_element_type=jnp.float32
        )
    cell_count = (
        features.shape[0] * lax.axis_size("dp") * length_x * features.shape[3] * features.shape[4]
    )
    grad_scale = 1.0 / math.sqrt(cell_count)
    summed = summed * grad_scale
    weight_count = taps * channels * channels
    return (
        hidden.astype(jnp.bfloat16),
        grad_in.astype(jnp.bfloat16),
        summed[:weight_count].reshape(taps, channels, channels),
        summed[weight_count:],
    )


def solution(mesh):
    in_specs = (
        P("dp", None, "gx", None, None),
        P("dp", None),
        P("dp", None),
        P(),
        P(),
        P("dp", None, "gx", None, None),
    )
    out_specs = (P("dp", None, "gx", None, None), P("dp", None, "gx", None, None), P(), P())
    return jax.shard_map(
        on_device, mesh=mesh, in_specs=in_specs, out_specs=out_specs, check_vma=False
    )
```

```python
import math

import jax
import jax.numpy as jnp
from jax import lax
from jax.sharding import PartitionSpec as P

tap_offsets = [
    (shift_x, shift_y, shift_z)
    for shift_x in range(3)
    for shift_y in range(3)
    for shift_z in range(3)
]


def shifted(value, axis, steps):
    count = lax.axis_size(axis)
    pairs = [(source, (source + steps) % count) for source in range(count)]
    return lax.ppermute(value, axis, pairs)


def neighbour_blocks(value, axis):
    count = lax.axis_size(axis)
    even = lax.axis_index(axis) % 2 == 0
    near = lax.ppermute(value, axis, [(s, s ^ 1) for s in range(count)])
    pairs = [(s, (s + 1) % count if s % 2 else (s - 1) % count) for s in range(count)]
    across = lax.ppermute(value, axis, pairs)
    return jnp.where(even, across, near), jnp.where(even, near, across)


def halo_planes(value, axis):
    count = lax.axis_size(axis)
    even = lax.axis_index(axis) % 2 == 0
    first, last = value[:, :, 0:1], value[:, :, -1:]
    near = lax.ppermute(jnp.where(even, last, first), axis, [(s, s ^ 1) for s in range(count)])
    pairs = [(s, (s + 1) % count if s % 2 else (s - 1) % count) for s in range(count)]
    across = lax.ppermute(jnp.where(even, first, last), axis, pairs)
    return jnp.where(even, across, near), jnp.where(even, near, across)


def butterfly_sum(value, axis):
    count = lax.axis_size(axis)
    step = count // 2
    while step >= 1:
        pairs = [(source, source ^ step) for source in range(count)]
        value = value + lax.ppermute(value, axis, pairs)
        step //= 2
    return value


def permute_axis(volume, offset, mirror_bit, dim_index):
    reverse = jnp.flip(volume, dim_index)
    return jnp.where(
        mirror_bit == 1,
        jnp.roll(reverse, -offset, axis=dim_index),
        jnp.roll(volume, offset, axis=dim_index),
    )


def augment_local(volume, offset, mirror_bits):
    volume = permute_axis(volume, offset[1], mirror_bits[1], 2)
    return permute_axis(volume, offset[2], mirror_bits[2], 3)


def gelu_parts(pre_act):
    normal_cdf = 0.5 * (1.0 + lax.erf(pre_act * 0.7071067811865476))
    density = jnp.exp(-0.5 * pre_act * pre_act) * 0.3989422804014327
    return (pre_act * normal_cdf, normal_cdf + pre_act * density)


def routed(pieces, axis, sign, constants):
    count = lax.axis_size(axis)
    here = lax.axis_index(axis)
    step = 1
    while step < count:
        pairs = [(peer, peer ^ step) for peer in range(count)]
        arrived = lax.ppermute(jnp.concatenate(pieces, axis=2), axis, pairs)
        updated = []
        begin = 0
        for piece, constant in zip(pieces, constants):
            size = piece.shape[2]
            wanted = jnp.mod(sign * (here - constant), 2 * step)
            take = (wanted // step % 2) != (here // step % 2)
            updated.append(jnp.where(take, arrived[:, :, begin : begin + size], piece))
            begin += size
        pieces = updated
        step *= 2
    return pieces


def on_device(features, offsets, flip_bits, weight, conv_bias, cotangent):
    planes = features.shape[2]
    devices_x = lax.axis_size("gx")
    length_x = planes * devices_x
    flip_x = flip_bits[0, 0] == 1
    effective = jnp.where(flip_x, jnp.mod(-offsets[0, 0], length_x), offsets[0, 0])
    coarse_steps = effective // planes
    remain = effective % planes
    sign = jnp.where(flip_x, -1, 1)
    constant = jnp.where(flip_x, devices_x - 1 + coarse_steps, coarse_steps)
    (raw,) = routed([features], "gx", sign, [constant])
    coarse = jnp.where(flip_x, jnp.flip(raw, 2), raw)
    before, after = neighbour_blocks(coarse, "gx")
    joined = jnp.concatenate([before, coarse, after[:, :, 0:1]], axis=2)
    window = lax.dynamic_slice_in_dim(joined, planes - 1 - remain, planes + 2, axis=2)
    padded = jax.vmap(augment_local)(window, offsets, flip_bits)

    taps = len(tap_offsets)
    channels = features.shape[1]
    kernel = weight.reshape(3, 3, 3, channels, channels)
    rolled = [(1 - e, 1 - h) for e in range(3) for h in range(3)]
    stacked_yz = jnp.concatenate([jnp.roll(padded, r, axis=(3, 4)) for r in rolled], axis=1)
    total = jnp.zeros(features.shape, jnp.float32) + conv_bias[None, :, None, None, None]
    for shift_x in range(3):
        window = stacked_yz[:, :, shift_x : shift_x + planes]
        mixed = jnp.transpose(kernel[shift_x], (2, 0, 1, 3)).reshape(channels, -1)
        total = total + jnp.einsum(
            "oc,bcxyz->boxyz", mixed, window, preferred_element_type=jnp.float32
        )
    hidden, slope = gelu_parts(total)
    grad_pre = (cotangent.astype(jnp.float32) * slope).astype(jnp.bfloat16)
    grad_before, grad_after = halo_planes(grad_pre, "gx")
    grad_list = []
    for shift_x in range(3):
        window = stacked_yz[:, :, shift_x : shift_x + planes]
        part = jnp.einsum("boxyz,bcxyz->oc", grad_pre, window, preferred_element_type=jnp.float32)
        part = jnp.transpose(part.reshape(channels, 3, 3, channels), (1, 2, 0, 3))
        grad_list.append(part.reshape(9, channels, channels))
    grad_b = jnp.sum(grad_pre.astype(jnp.float32), axis=(0, 2, 3, 4))
    stacked = jnp.concatenate([jnp.concatenate(grad_list, axis=0).reshape(-1), grad_b])
    summed = butterfly_sum(butterfly_sum(stacked, "gx"), "dp")
    grad_pad = jnp.concatenate([grad_before, grad_pre, grad_after], axis=2)
    rolled_back = [(e - 1, h - 1) for e in range(3) for h in range(3)]
    grad_yz = jnp.concatenate([jnp.roll(grad_pad, r, axis=(3, 4)) for r in rolled_back], axis=1)
    grad_in = jnp.zeros(features.shape, jnp.float32)
    for shift_x in range(3):
        moved_grad = grad_yz[:, :, 2 - shift_x : 2 - shift_x + planes]
        mixed = kernel[shift_x].reshape(-1, channels)
        grad_in = grad_in + jnp.einsum(
            "ci,bcxyz->bixyz", mixed, moved_grad, preferred_element_type=jnp.float32
        )
    cell_count = (
        features.shape[0] * lax.axis_size("dp") * length_x * features.shape[3] * features.shape[4]
    )
    grad_scale = 1.0 / math.sqrt(cell_count)
    summed = summed * grad_scale
    weight_count = taps * channels * channels
    return (
        hidden.astype(jnp.bfloat16),
        grad_in.astype(jnp.bfloat16),
        summed[:weight_count].reshape(taps, channels, channels),
        summed[weight_count:],
    )


def solution(mesh):
    in_specs = (
        P("dp", None, "gx", None, None),
        P("dp", None),
        P("dp", None),
        P(),
        P(),
        P("dp", None, "gx", None, None),
    )
    out_specs = (P("dp", None, "gx", None, None), P("dp", None, "gx", None, None), P(), P())
    return jax.shard_map(
        on_device, mesh=mesh, in_specs=in_specs, out_specs=out_specs, check_vma=False
    )
```

```python
import math

import jax
import jax.numpy as jnp
from jax import lax
from jax.sharding import PartitionSpec as P

tap_offsets = [
    (shift_x, shift_y, shift_z)
    for shift_x in range(3)
    for shift_y in range(3)
    for shift_z in range(3)
]


def shifted(value, axis, steps):
    count = lax.axis_size(axis)
    pairs = [(source, (source + steps) % count) for source in range(count)]
    return lax.ppermute(value, axis, pairs)


def neighbour_blocks(value, axis):
    count = lax.axis_size(axis)
    even = lax.axis_index(axis) % 2 == 0
    near = lax.ppermute(value, axis, [(s, s ^ 1) for s in range(count)])
    pairs = [(s, (s + 1) % count if s % 2 else (s - 1) % count) for s in range(count)]
    across = lax.ppermute(value, axis, pairs)
    return jnp.where(even, across, near), jnp.where(even, near, across)


def halo_planes(value, axis):
    count = lax.axis_size(axis)
    even = lax.axis_index(axis) % 2 == 0
    first, last = value[:, :, 0:1], value[:, :, -1:]
    near = lax.ppermute(jnp.where(even, last, first), axis, [(s, s ^ 1) for s in range(count)])
    pairs = [(s, (s + 1) % count if s % 2 else (s - 1) % count) for s in range(count)]
    across = lax.ppermute(jnp.where(even, first, last), axis, pairs)
    return jnp.where(even, across, near), jnp.where(even, near, across)


def butterfly_sum(value, axis):
    count = lax.axis_size(axis)
    step = count // 2
    while step >= 1:
        pairs = [(source, source ^ step) for source in range(count)]
        value = value + lax.ppermute(value, axis, pairs)
        step //= 2
    return value


def permute_axis(volume, offset, mirror_bit, dim_index):
    reverse = jnp.flip(volume, dim_index)
    return jnp.where(
        mirror_bit == 1,
        jnp.roll(reverse, -offset, axis=dim_index),
        jnp.roll(volume, offset, axis=dim_index),
    )


def augment_local(volume, offset, mirror_bits):
    volume = permute_axis(volume, offset[1], mirror_bits[1], 2)
    return permute_axis(volume, offset[2], mirror_bits[2], 3)


def gelu_parts(pre_act):
    normal_cdf = 0.5 * (1.0 + lax.erf(pre_act * 0.7071067811865476))
    density = jnp.exp(-0.5 * pre_act * pre_act) * 0.3989422804014327
    return (pre_act * normal_cdf, normal_cdf + pre_act * density)


def routed(pieces, axis, sign, constants):
    count = lax.axis_size(axis)
    here = lax.axis_index(axis)
    step = 1
    while step < count:
        pairs = [(peer, peer ^ step) for peer in range(count)]
        arrived = lax.ppermute(jnp.concatenate(pieces, axis=2), axis, pairs)
        updated = []
        begin = 0
        for piece, constant in zip(pieces, constants):
            size = piece.shape[2]
            wanted = jnp.mod(sign * (here - constant), 2 * step)
            take = (wanted // step % 2) != (here // step % 2)
            updated.append(jnp.where(take, arrived[:, :, begin : begin + size], piece))
            begin += size
        pieces = updated
        step *= 2
    return pieces


def on_device(features, offsets, flip_bits, weight, conv_bias, cotangent):
    planes = features.shape[2]
    devices_x = lax.axis_size("gx")
    length_x = planes * devices_x
    flip_x = flip_bits[0, 0] == 1
    effective = jnp.where(flip_x, jnp.mod(-offsets[0, 0], length_x), offsets[0, 0])
    coarse_steps = effective // planes
    remain = effective % planes
    sign = jnp.where(flip_x, -1, 1)
    constant = jnp.where(flip_x, devices_x - 1 + coarse_steps, coarse_steps)
    (raw,) = routed([features], "gx", sign, [constant])
    coarse = jnp.where(flip_x, jnp.flip(raw, 2), raw)
    before, after = neighbour_blocks(coarse, "gx")
    joined = jnp.concatenate([before, coarse, after[:, :, 0:1]], axis=2)
    window = lax.dynamic_slice_in_dim(joined, planes - 1 - remain, planes + 2, axis=2)
    padded = jax.vmap(augment_local)(window, offsets, flip_bits)

    taps = len(tap_offsets)
    channels = features.shape[1]
    kernel = weight.reshape(3, 3, 3, channels, channels)
    rolled = [(1 - e, 1 - h) for e in range(3) for h in range(3)]
    stacked_yz = jnp.concatenate([jnp.roll(padded, r, axis=(3, 4)) for r in rolled], axis=1)
    total = jnp.zeros(features.shape, jnp.float32) + conv_bias[None, :, None, None, None]
    for shift_x in range(3):
        window = stacked_yz[:, :, shift_x : shift_x + planes]
        mixed = jnp.transpose(kernel[shift_x], (2, 0, 1, 3)).reshape(channels, -1)
        total = total + jnp.einsum(
            "oc,bcxyz->boxyz", mixed, window, preferred_element_type=jnp.float32
        )
    hidden, slope = gelu_parts(total)
    grad_pre = (cotangent.astype(jnp.float32) * slope).astype(jnp.bfloat16)
    grad_before, grad_after = halo_planes(grad_pre, "gx")
    grad_list = []
    for shift_x in range(3):
        window = stacked_yz[:, :, shift_x : shift_x + planes]
        part = jnp.einsum("bcxyz,boxyz->co", window, grad_pre, preferred_element_type=jnp.float32)
        part = jnp.transpose(part.reshape(3, 3, channels, channels), (0, 1, 3, 2))
        grad_list.append(part.reshape(9, channels, channels))
    grad_b = jnp.sum(grad_pre.astype(jnp.float32), axis=(0, 2, 3, 4))
    stacked = jnp.concatenate([jnp.concatenate(grad_list, axis=0).reshape(-1), grad_b])
    summed = butterfly_sum(butterfly_sum(stacked, "gx"), "dp")
    grad_pad = jnp.concatenate([grad_before, grad_pre, grad_after], axis=2)
    rolled_back = [(e - 1, h - 1) for e in range(3) for h in range(3)]
    grad_yz = jnp.concatenate([jnp.roll(grad_pad, r, axis=(3, 4)) for r in rolled_back], axis=1)
    grad_in = jnp.zeros(features.shape, jnp.float32)
    for shift_x in range(3):
        moved_grad = grad_yz[:, :, 2 - shift_x : 2 - shift_x + planes]
        mixed = kernel[shift_x].reshape(-1, channels)
        grad_in = grad_in + jnp.einsum(
            "ci,bcxyz->bixyz", mixed, moved_grad, preferred_element_type=jnp.float32
        )
    cell_count = (
        features.shape[0] * lax.axis_size("dp") * length_x * features.shape[3] * features.shape[4]
    )
    grad_scale = 1.0 / math.sqrt(cell_count)
    summed = summed * grad_scale
    weight_count = taps * channels * channels
    return (
        hidden.astype(jnp.bfloat16),
        grad_in.astype(jnp.bfloat16),
        summed[:weight_count].reshape(taps, channels, channels),
        summed[weight_count:],
    )


def solution(mesh):
    in_specs = (
        P("dp", None, "gx", None, None),
        P("dp", None),
        P("dp", None),
        P(),
        P(),
        P("dp", None, "gx", None, None),
    )
    out_specs = (P("dp", None, "gx", None, None), P("dp", None, "gx", None, None), P(), P())
    return jax.shard_map(
        on_device, mesh=mesh, in_specs=in_specs, out_specs=out_specs, check_vma=False
    )
```

```python
import math

import jax
import jax.numpy as jnp
from jax import lax
from jax.sharding import PartitionSpec as P

tap_offsets = [
    (shift_x, shift_y, shift_z)
    for shift_x in range(3)
    for shift_y in range(3)
    for shift_z in range(3)
]


def shifted(value, axis, steps):
    count = lax.axis_size(axis)
    pairs = [(source, (source + steps) % count) for source in range(count)]
    return lax.ppermute(value, axis, pairs)


def neighbour_blocks(value, axis):
    count = lax.axis_size(axis)
    even = lax.axis_index(axis) % 2 == 0
    near = lax.ppermute(value, axis, [(s, s ^ 1) for s in range(count)])
    pairs = [(s, (s + 1) % count if s % 2 else (s - 1) % count) for s in range(count)]
    across = lax.ppermute(value, axis, pairs)
    return jnp.where(even, across, near), jnp.where(even, near, across)


def halo_planes(value, axis):
    count = lax.axis_size(axis)
    even = lax.axis_index(axis) % 2 == 0
    first, last = value[:, :, 0:1], value[:, :, -1:]
    near = lax.ppermute(jnp.where(even, last, first), axis, [(s, s ^ 1) for s in range(count)])
    pairs = [(s, (s + 1) % count if s % 2 else (s - 1) % count) for s in range(count)]
    across = lax.ppermute(jnp.where(even, first, last), axis, pairs)
    return jnp.where(even, across, near), jnp.where(even, near, across)


def butterfly_sum(value, axis):
    count = lax.axis_size(axis)
    step = count // 2
    while step >= 1:
        pairs = [(source, source ^ step) for source in range(count)]
        value = value + lax.ppermute(value, axis, pairs)
        step //= 2
    return value


def permute_axis(volume, offset, mirror_bit, dim_index):
    reverse = jnp.flip(volume, dim_index)
    return jnp.where(
        mirror_bit == 1,
        jnp.roll(reverse, -offset, axis=dim_index),
        jnp.roll(volume, offset, axis=dim_index),
    )


def augment_local(volume, offset, mirror_bits):
    volume = permute_axis(volume, offset[1], mirror_bits[1], 2)
    return permute_axis(volume, offset[2], mirror_bits[2], 3)


def gelu_parts(pre_act):
    normal_cdf = 0.5 * (1.0 + lax.erf(pre_act * 0.7071067811865476))
    density = jnp.exp(-0.5 * pre_act * pre_act) * 0.3989422804014327
    return (pre_act * normal_cdf, normal_cdf + pre_act * density)


def routed(pieces, axis, sign, constants):
    count = lax.axis_size(axis)
    here = lax.axis_index(axis)
    step = 1
    while step < count:
        pairs = [(peer, peer ^ step) for peer in range(count)]
        arrived = lax.ppermute(jnp.concatenate(pieces, axis=2), axis, pairs)
        updated = []
        begin = 0
        for piece, constant in zip(pieces, constants):
            size = piece.shape[2]
            wanted = jnp.mod(sign * (here - constant), 2 * step)
            take = (wanted // step % 2) != (here // step % 2)
            updated.append(jnp.where(take, arrived[:, :, begin : begin + size], piece))
            begin += size
        pieces = updated
        step *= 2
    return pieces


def on_device(features, offsets, flip_bits, weight, conv_bias, cotangent):
    planes = features.shape[2]
    devices_x = lax.axis_size("gx")
    length_x = planes * devices_x
    flip_x = flip_bits[0, 0] == 1
    effective = jnp.where(flip_x, jnp.mod(-offsets[0, 0], length_x), offsets[0, 0])
    coarse_steps = effective // planes
    remain = effective % planes
    sign = jnp.where(flip_x, -1, 1)
    constant = jnp.where(flip_x, devices_x - 1 + coarse_steps, coarse_steps)
    (raw,) = routed([features], "gx", sign, [constant])
    coarse = jnp.where(flip_x, jnp.flip(raw, 2), raw)
    before, after = neighbour_blocks(coarse, "gx")
    joined = jnp.concatenate([before, coarse, after[:, :, 0:1]], axis=2)
    window = lax.dynamic_slice_in_dim(joined, planes - 1 - remain, planes + 2, axis=2)
    padded = jax.vmap(augment_local)(window, offsets, flip_bits)

    taps = len(tap_offsets)
    channels = features.shape[1]
    kernel = weight.reshape(3, 3, 3, channels, channels)
    rolled = [(1 - e, 1 - h) for e in range(3) for h in range(3)]
    stacked_yz = jnp.concatenate([jnp.roll(padded, r, axis=(3, 4)) for r in rolled], axis=1)
    total = jnp.zeros(features.shape, jnp.float32) + conv_bias[None, :, None, None, None]
    for shift_x in range(3):
        window = stacked_yz[:, :, shift_x : shift_x + planes]
        mixed = jnp.transpose(kernel[shift_x], (2, 0, 1, 3)).reshape(channels, -1)
        total = total + jnp.einsum(
            "bcxyz,oc->boxyz", window, mixed, preferred_element_type=jnp.float32
        )
    hidden, slope = gelu_parts(total)
    grad_pre = (cotangent.astype(jnp.float32) * slope).astype(jnp.bfloat16)
    grad_before, grad_after = halo_planes(grad_pre, "gx")
    grad_list = []
    for shift_x in range(3):
        window = stacked_yz[:, :, shift_x : shift_x + planes]
        part = jnp.einsum("bcxyz,boxyz->co", window, grad_pre, preferred_element_type=jnp.float32)
        part = jnp.transpose(part.reshape(3, 3, channels, channels), (0, 1, 3, 2))
        grad_list.append(part.reshape(9, channels, channels))
    grad_b = jnp.sum(grad_pre.astype(jnp.float32), axis=(0, 2, 3, 4))
    stacked = jnp.concatenate([jnp.concatenate(grad_list, axis=0).reshape(-1), grad_b])
    summed = butterfly_sum(butterfly_sum(stacked, "gx"), "dp")
    grad_pad = jnp.concatenate([grad_before, grad_pre, grad_after], axis=2)
    rolled_back = [(e - 1, h - 1) for e in range(3) for h in range(3)]
    grad_yz = jnp.concatenate([jnp.roll(grad_pad, r, axis=(3, 4)) for r in rolled_back], axis=1)
    grad_in = jnp.zeros(features.shape, jnp.float32)
    for shift_x in range(3):
        moved_grad = grad_yz[:, :, 2 - shift_x : 2 - shift_x + planes]
        mixed = kernel[shift_x].reshape(-1, channels)
        grad_in = grad_in + jnp.einsum(
            "ci,bcxyz->bixyz", mixed, moved_grad, preferred_element_type=jnp.float32
        )
    cell_count = (
        features.shape[0] * lax.axis_size("dp") * length_x * features.shape[3] * features.shape[4]
    )
    grad_scale = 1.0 / math.sqrt(cell_count)
    summed = summed * grad_scale
    weight_count = taps * channels * channels
    return (
        hidden.astype(jnp.bfloat16),
        grad_in.astype(jnp.bfloat16),
        summed[:weight_count].reshape(taps, channels, channels),
        summed[weight_count:],
    )


def solution(mesh):
    in_specs = (
        P("dp", None, "gx", None, None),
        P("dp", None),
        P("dp", None),
        P(),
        P(),
        P("dp", None, "gx", None, None),
    )
    out_specs = (P("dp", None, "gx", None, None), P("dp", None, "gx", None, None), P(), P())
    return jax.shard_map(
        on_device, mesh=mesh, in_specs=in_specs, out_specs=out_specs, check_vma=False
    )
```

```python
import math

import jax
import jax.numpy as jnp
from jax import lax
from jax.sharding import PartitionSpec as P

tap_offsets = [
    (shift_x, shift_y, shift_z)
    for shift_x in range(3)
    for shift_y in range(3)
    for shift_z in range(3)
]


def shifted(value, axis, steps):
    count = lax.axis_size(axis)
    pairs = [(source, (source + steps) % count) for source in range(count)]
    return lax.ppermute(value, axis, pairs)


def neighbour_blocks(value, axis):
    count = lax.axis_size(axis)
    even = lax.axis_index(axis) % 2 == 0
    near = lax.ppermute(value, axis, [(s, s ^ 1) for s in range(count)])
    pairs = [(s, (s + 1) % count if s % 2 else (s - 1) % count) for s in range(count)]
    across = lax.ppermute(value, axis, pairs)
    return jnp.where(even, across, near), jnp.where(even, near, across)


def halo_planes(value, axis):
    count = lax.axis_size(axis)
    even = lax.axis_index(axis) % 2 == 0
    first, last = value[:, :, 0:1], value[:, :, -1:]
    near = lax.ppermute(jnp.where(even, last, first), axis, [(s, s ^ 1) for s in range(count)])
    pairs = [(s, (s + 1) % count if s % 2 else (s - 1) % count) for s in range(count)]
    across = lax.ppermute(jnp.where(even, first, last), axis, pairs)
    return jnp.where(even, across, near), jnp.where(even, near, across)


def butterfly_sum(value, axis):
    count = lax.axis_size(axis)
    step = count // 2
    while step >= 1:
        pairs = [(source, source ^ step) for source in range(count)]
        value = value + lax.ppermute(value, axis, pairs)
        step //= 2
    return value


def permute_axis(volume, offset, mirror_bit, dim_index):
    reverse = jnp.flip(volume, dim_index)
    return jnp.where(
        mirror_bit == 1,
        jnp.roll(reverse, -offset, axis=dim_index),
        jnp.roll(volume, offset, axis=dim_index),
    )


def augment_local(volume, offset, mirror_bits):
    volume = permute_axis(volume, offset[1], mirror_bits[1], 2)
    return permute_axis(volume, offset[2], mirror_bits[2], 3)


def gelu_parts(pre_act):
    normal_cdf = 0.5 * (1.0 + lax.erf(pre_act * 0.7071067811865476))
    density = jnp.exp(-0.5 * pre_act * pre_act) * 0.3989422804014327
    return (pre_act * normal_cdf, normal_cdf + pre_act * density)


def routed(pieces, axis, sign, constants):
    count = lax.axis_size(axis)
    here = lax.axis_index(axis)
    step = 1
    while step < count:
        pairs = [(peer, peer ^ step) for peer in range(count)]
        arrived = lax.ppermute(jnp.concatenate(pieces, axis=2), axis, pairs)
        updated = []
        begin = 0
        for piece, constant in zip(pieces, constants):
            size = piece.shape[2]
            wanted = jnp.mod(sign * (here - constant), 2 * step)
            take = (wanted // step % 2) != (here // step % 2)
            updated.append(jnp.where(take, arrived[:, :, begin : begin + size], piece))
            begin += size
        pieces = updated
        step *= 2
    return pieces


def on_device(features, offsets, flip_bits, weight, conv_bias, cotangent):
    planes = features.shape[2]
    devices_x = lax.axis_size("gx")
    length_x = planes * devices_x
    flip_x = flip_bits[0, 0] == 1
    effective = jnp.where(flip_x, jnp.mod(-offsets[0, 0], length_x), offsets[0, 0])
    coarse_steps = effective // planes
    remain = effective % planes
    sign = jnp.where(flip_x, -1, 1)
    constant = jnp.where(flip_x, devices_x - 1 + coarse_steps, coarse_steps)
    (raw,) = routed([features], "gx", sign, [constant])
    coarse = jnp.where(flip_x, jnp.flip(raw, 2), raw)
    before, after = neighbour_blocks(coarse, "gx")
    joined = jnp.concatenate([before, coarse, after[:, :, 0:1]], axis=2)
    window = lax.dynamic_slice_in_dim(joined, planes - 1 - remain, planes + 2, axis=2)
    padded = jax.vmap(augment_local)(window, offsets, flip_bits)

    taps = len(tap_offsets)
    channels = features.shape[1]
    kernel = weight.reshape(3, 3, 3, channels, channels)
    rolled = [(1 - e, 1 - h) for e in range(3) for h in range(3)]
    stacked_yz = jnp.concatenate([jnp.roll(padded, r, axis=(3, 4)) for r in rolled], axis=1)
    total = jnp.zeros(features.shape, jnp.float32) + conv_bias[None, :, None, None, None]
    for shift_x in range(3):
        window = stacked_yz[:, :, shift_x : shift_x + planes]
        mixed = jnp.transpose(kernel[shift_x], (2, 0, 1, 3)).reshape(channels, -1)
        total = total + jnp.einsum(
            "bcxyz,oc->boxyz", window, mixed, preferred_element_type=jnp.float32
        )
    hidden, slope = gelu_parts(total)
    grad_pre = (cotangent.astype(jnp.float32) * slope).astype(jnp.bfloat16)
    grad_before, grad_after = halo_planes(grad_pre, "gx")
    grad_list = []
    for shift_x in range(3):
        window = stacked_yz[:, :, shift_x : shift_x + planes]
        part = jnp.einsum("bcxyz,boxyz->co", window, grad_pre, preferred_element_type=jnp.float32)
        part = jnp.transpose(part.reshape(3, 3, channels, channels), (0, 1, 3, 2))
        grad_list.append(part.reshape(9, channels, channels))
    grad_b = jnp.sum(grad_pre.astype(jnp.float32), axis=(0, 2, 3, 4))
    stacked = jnp.concatenate([jnp.concatenate(grad_list, axis=0).reshape(-1), grad_b])
    summed = butterfly_sum(butterfly_sum(stacked, "dp"), "gx")
    grad_pad = jnp.concatenate([grad_before, grad_pre, grad_after], axis=2)
    rolled_back = [(e - 1, h - 1) for e in range(3) for h in range(3)]
    grad_yz = jnp.concatenate([jnp.roll(grad_pad, r, axis=(3, 4)) for r in rolled_back], axis=1)
    grad_in = jnp.zeros(features.shape, jnp.float32)
    for shift_x in range(3):
        moved_grad = grad_yz[:, :, 2 - shift_x : 2 - shift_x + planes]
        mixed = kernel[shift_x].reshape(-1, channels)
        grad_in = grad_in + jnp.einsum(
            "ci,bcxyz->bixyz", mixed, moved_grad, preferred_element_type=jnp.float32
        )
    cell_count = (
        features.shape[0] * lax.axis_size("dp") * length_x * features.shape[3] * features.shape[4]
    )
    grad_scale = 1.0 / math.sqrt(cell_count)
    summed = summed * grad_scale
    weight_count = taps * channels * channels
    return (
        hidden.astype(jnp.bfloat16),
        grad_in.astype(jnp.bfloat16),
        summed[:weight_count].reshape(taps, channels, channels),
        summed[weight_count:],
    )


def solution(mesh):
    in_specs = (
        P("dp", None, "gx", None, None),
        P("dp", None),
        P("dp", None),
        P(),
        P(),
        P("dp", None, "gx", None, None),
    )
    out_specs = (P("dp", None, "gx", None, None), P("dp", None, "gx", None, None), P(), P())
    return jax.shard_map(
        on_device, mesh=mesh, in_specs=in_specs, out_specs=out_specs, check_vma=False
    )
```
